128 devices in a mesh: tok: 16 (over y, z), own: 8 (over x, core).
Axes of the slice: x: 4, y: 4, z: 4, core: 2. Of those that a mesh axis runs over, the one named last changes fastest.
Arguments:
- tokens: bfloat16 [16384, 1152], P(('tok', 'own')), may hold values from -6 to 6
- norm_gain: bfloat16 [1152], replicated, may hold values from 0.099609375 to 1.8984375
- w_query: bfloat16 [1152, 1152], replicated, as said below
- w_key: bfloat16 [1152, 384], replicated, as said below
- w_value: bfloat16 [1152, 384], replicated, may hold values from -0.1875 to 0.1875
- w_output: bfloat16 [1152, 1152], replicated, may hold values from -0.1875 to 0.1875
- qkv_in: bfloat16 [64, 48, 1152], P('own', None, 'tok'), may hold values from -0.1875 to 0.1875
- q_out: bfloat16 [64, 16, 1152], P('own', None, 'tok'), may hold values from -1.5 to 1.5
- kv_out: bfloat16 [64, 32, 384], P('own', None, 'tok'), may hold values from -1.5 to 1.5
- o_in: bfloat16 [64, 16, 1152], P('own', None, 'tok'), may hold values from -0.1875 to 0.1875
- o_out: bfloat16 [64, 16, 1152], P('own', None, 'tok'), may hold values from -1.5 to 1.5
- lengths: int32 [64], replicated, may hold values from 32 to 1536, as said below
- prompt_adapter: int32 [64], replicated, may hold values from 0 to 63
- adapter_slot: int32 [64], replicated, may hold values from 0 to 63, each once
Outputs:
- mixed: bfloat16 [16384, 1152], P(('tok', 'own'))
- kv_cache: bfloat16 [16384, 768], P(('tok', 'own'))
The draws below stay inside these ranges and needn't reach their ends.
Inputs may be any that keep to these rules, and one draw needn't show every extreme that they name: `w_query`: entries lie within 6 / sqrt(1152) of zero. `w_key`: entries lie within 6 / sqrt(1152) of zero. `lengths`: lengths sum to 16384; exactly 8 prompts are 1536 long; the others hold 32 to 128 tokens, and one of them exactly 32. `adapter_slot`: each slot appears once; slot s is row s of the adapter tables, held by own index s // 8.
All inputs are finite; a program needn't handle non-finite values.
Results may differ from the reference program's by a relative error of at most 0.02.
Values may be sent and summed in bfloat16 or wider, within the bound.
No kernel may reach another device: no remote copies, remote signals or barrier semaphores. Data moves between devices by JAX's collectives and lax.ppermute only.
A program may use at most 128 MiB of HBM per device.

```python
import math
import jax
import jax.numpy as jnp
import numpy as np
from jax import lax

D = 1152
HEADS = 18
KV_HEADS = 6
HEAD_WIDTH = 64
RANK = 16
ADAPTERS = 64
TOK_DEV = 128
REACH = 12
KVW = 384
LONG = 1536
SHORT_MIN = 32
SHORT_MAX = 128
TOKENS = 16384
PROMPTS = 64
LONGS = 8
SHORTS = 56


def draw_tokens(key, part):
    values = jax.random.truncated_normal(jax.random.fold_in(key, 9204), -6.0, 6.0, (TOKENS, D), jnp.float32)
    return values.astype(jnp.bfloat16)


def draw_w_query(key, part):
    values = jax.random.truncated_normal(jax.random.fold_in(key, 9302), -6.0, 6.0, (D, D), jnp.float32) / math.sqrt(D)
    return values.astype(jnp.bfloat16)


def draw_w_key(key, part):
    values = jax.random.truncated_normal(jax.random.fold_in(key, 9402), -6.0, 6.0, (D, KVW), jnp.float32) / math.sqrt(D)
    return values.astype(jnp.bfloat16)


def draw_lengths(key, part):
    room = SHORT_MAX - SHORT_MIN
    spare_total = TOKENS - LONGS * LONG - SHORTS * SHORT_MIN
    cell_count = (SHORTS - 1) * room
    slot_order = jax.random.permutation(jax.random.fold_in(key, 9501), cell_count).astype(jnp.int32)
    cell_of = 1 + slot_order[:spare_total] // room
    short_ids = jnp.arange(SHORTS, dtype=jnp.int32)
    extra_tokens = jnp.sum((cell_of[:, None] == short_ids[None, :]).astype(jnp.int32), axis=0)
    short_lengths = SHORT_MIN + extra_tokens
    prompt_role = jax.random.permutation(jax.random.fold_in(key, 9502), PROMPTS).astype(jnp.int32)
    short_index = jnp.clip(prompt_role - LONGS, 0, SHORTS - 1)
    lengths = jnp.where(prompt_role < LONGS, LONG, jnp.take(short_lengths, short_index))
    return lengths.astype(jnp.int32)


def place_ends(entries, rng, least, top_value):
    longest = entries.shape.index(max(entries.shape))
    spots = []
    for shift in (0, 1):
        where = [jax.random.randint(jax.random.fold_in(rng, axis), (), 0, length) for axis, length in enumerate(entries.shape)]
        where[longest] = (where[longest] + shift) % entries.shape[longest]
        spots.append(tuple(where))
    return entries.at[spots[0]].set(least).at[spots[1]].set(top_value)


def block_scale(own_key, extent, shards, least, top_value):
    def one(dim, parts):
        draws = jax.random.uniform(jax.random.fold_in(jax.random.fold_in(own_key, 6), dim), (parts,), jnp.float32, least / len(shards), top_value / len(shards))
        return jnp.repeat(jnp.exp(draws), extent[dim] // parts).reshape((-1,) + (1,) * (len(extent) - dim - 1))

    level = one(*shards[0])
    for cut in shards[1:]:
        level = level * one(*cut)
    return level


def cumulative_ranks(amount, lean):
    weights = [(1 << 20) // math.isqrt(rank ** lean) + 1 for rank in range(1, amount + 1)]
    scale = 1 + sum(weights) // (1 << 30)
    return np.cumsum(np.array([max(1, weight // scale) for weight in weights]))


def ranked(rng, shape, amount, lean):
    listing = cumulative_ranks(amount, lean)
    lot = jax.random.randint(jax.random.fold_in(rng, 1), shape, 0, int(listing[amount - 1]))
    grade = jnp.searchsorted(jnp.asarray(listing, jnp.int32), lot, side="right")
    return jax.random.permutation(jax.random.fold_in(rng, 2), amount)[grade].astype(jnp.int32)


def scatter_about(key, shape, deviation, bound, shards=(), kind=jnp.bfloat16):
    drawn = jax.random.normal(key, shape, jnp.float32) * deviation
    if len(shards) > 0:
        drawn = block_scale(key, shape, shards, -0.22, 0.18) * drawn
    return jnp.clip(drawn, min=-bound, max=bound).astype(kind)


def setup_inputs(seed: int = 0) -> dict:
    seeds = jax.random.split(jax.random.key(seed), 15)
    tokens = draw_tokens(jax.random.fold_in(seeds[14], 71), 0)
    norm_gain = jnp.clip(1.0 + 0.18 * jax.random.normal(seeds[1], (D,), jnp.float32), 0.099609375, 1.8984375).astype(jnp.bfloat16)
    w_query = draw_w_query(jax.random.fold_in(seeds[14], 71), 0)
    w_key = draw_w_key(jax.random.fold_in(seeds[14], 71), 0)
    w_value = scatter_about(seeds[4], (D, KVW), D ** -0.5, 0.1875)
    w_output = scatter_about(seeds[5], (D, D), D ** -0.5, 0.1875)
    qkv_in = scatter_about(seeds[6], (ADAPTERS, 3 * RANK, D), D ** -0.5, 0.1875, ((0, 8), (2, 16)))
    q_out = scatter_about(seeds[7], (ADAPTERS, RANK, D), RANK ** -0.5, 1.5, ((0, 8), (2, 16)))
    kv_out = scatter_about(seeds[8], (ADAPTERS, 2 * RANK, KVW), RANK ** -0.5, 1.5, ((0, 8), (2, 16)))
    o_in = scatter_about(seeds[9], (ADAPTERS, RANK, D), D ** -0.5, 0.1875, ((0, 8), (2, 16)))
    o_out = scatter_about(seeds[10], (ADAPTERS, RANK, D), RANK ** -0.5, 1.5, ((0, 8), (2, 16)))
    lengths = draw_lengths(jax.random.fold_in(seeds[14], 71), 0)
    prompt_adapter = place_ends(ranked(seeds[12], (PROMPTS,), ADAPTERS, 2), jax.random.fold_in(seeds[12], 3), 0, ADAPTERS - 1).astype(jnp.int32)
    adapter_slot = jax.random.permutation(seeds[13], ADAPTERS).astype(jnp.int32)
    return {"tokens": tokens, "norm_gain": norm_gain, "w_query": w_query, "w_key": w_key, "w_value": w_value, "w_output": w_output, "qkv_in": qkv_in, "q_out": q_out, "kv_out": kv_out, "o_in": o_in, "o_out": o_out, "lengths": lengths, "prompt_adapter": prompt_adapter, "adapter_slot": adapter_slot}


EPS = 1e-05
THETA = 10000.0

def rms_norm(row_block, gain_vec):
    widened = row_block.astype(jnp.float32)
    inverse_rms = lax.rsqrt(lax.optimization_barrier(jnp.mean(widened * widened, axis=-1, keepdims=True)) + EPS)
    return (widened * inverse_rms * gain_vec.astype(jnp.float32)).astype(jnp.bfloat16)

def prompt_index(positions, lengths):
    prompt_ends = jnp.cumsum(lengths).astype(jnp.int32)
    prompt_starts = prompt_ends - lengths
    inside = (positions[:, None] >= prompt_starts[None, :]).astype(jnp.int32)
    segment = lax.optimization_barrier(jnp.sum(inside, axis=1)) - 1
    members = jnp.arange(lengths.shape[0], dtype=jnp.int32)[None, :] == segment[:, None]
    offset = positions - lax.optimization_barrier(jnp.sum(jnp.where(members, prompt_starts[None, :], 0), axis=1))
    return (segment, offset, members)

def slot_lookup(adapter, adapter_slot):
    matches = jnp.arange(adapter_slot.shape[0], dtype=jnp.int32)[None, :] == adapter[:, None]
    return lax.optimization_barrier(jnp.sum(jnp.where(matches, adapter_slot[None, :], 0), axis=1))

def rotate(vectors, offset):
    half_dim = vectors.shape[-1] // 2
    frequency = jnp.exp(jnp.arange(half_dim, dtype=jnp.float32) * (-2.0 * math.log(THETA) / vectors.shape[-1]))
    angles = offset.astype(jnp.float32)[:, None] * frequency[None, :]
    cosine = jnp.cos(angles)[:, None, :]
    sine_table = jnp.sin(angles)[:, None, :]
    first_half = vectors[..., :half_dim]
    second_half = vectors[..., half_dim:]
    return jnp.concatenate([first_half * cosine - second_half * sine_table, second_half * cosine + first_half * sine_table], axis=-1)

def adapter_terms(row_block, slot_block, a_in, pieces):
    chosen_in = jnp.take(a_in, slot_block, axis=0).astype(jnp.float32)
    projected = jnp.einsum('nd,nrd->nr', row_block.astype(jnp.float32), chosen_in)
    low_rank = lax.optimization_barrier(projected.astype(jnp.bfloat16)).astype(jnp.float32)
    results = []
    for col_start, b_table in pieces:
        chosen_out = jnp.take(b_table, slot_block, axis=0).astype(jnp.float32)
        section = low_rank[:, col_start:col_start + b_table.shape[1]]
        results.append(jnp.einsum('nr,nro->no', section, chosen_out).astype(jnp.bfloat16))
    return results

def attend(query_block, window, allowed):
    count_rows = query_block.shape[0]
    key_count = window.shape[0]
    groups = HEADS // KV_HEADS
    query_head_rows = query_block.astype(jnp.float32).reshape(count_rows, KV_HEADS, groups, HEAD_WIDTH)
    key_head_rows = window[:, :KVW].astype(jnp.float32).reshape(key_count, KV_HEADS, HEAD_WIDTH)
    value_head_rows = window[:, KVW:].astype(jnp.float32).reshape(key_count, KV_HEADS, HEAD_WIDTH)
    score_matrix = jnp.einsum('qkzr,ckr->kzqc', query_head_rows, key_head_rows) * HEAD_WIDTH ** (-0.5)
    score_matrix = jnp.where(allowed[None, None], score_matrix, -1e+30)
    top_score = lax.optimization_barrier(jnp.max(score_matrix, axis=-1, keepdims=True))
    exp_scores = jnp.exp(score_matrix - top_score)
    row_total = lax.optimization_barrier(jnp.sum(exp_scores, axis=-1))
    rounded_values = lax.optimization_barrier(exp_scores.astype(jnp.bfloat16)).astype(jnp.float32)
    summed_rows = jnp.einsum('iyxv,vip->xiyp', rounded_values, value_head_rows)
    attended = summed_rows / jnp.transpose(row_total, (2, 0, 1))[..., None]
    return attended.reshape(count_rows, D).astype(jnp.bfloat16)

def reference(tokens, norm_gain, w_query, w_key, w_value, w_output, qkv_in, q_out, kv_out, o_in, o_out, lengths, prompt_adapter, adapter_slot):
    positions = jnp.arange(TOKENS, dtype=jnp.int32)
    segment, offset, members = prompt_index(positions, lengths)
    adapter = lax.optimization_barrier(jnp.sum(jnp.where(members, prompt_adapter[None, :], 0), axis=1))
    slot_of = slot_lookup(adapter, adapter_slot)
    normed = rms_norm(tokens, norm_gain)
    blocks = TOKENS // TOK_DEV

    def project(inputs):
        normed_block, slot_block, offset_block = inputs
        count_rows = normed_block.shape[0]
        delta_q, delta_k, delta_v = adapter_terms(normed_block, slot_block, qkv_in, ((0, q_out), (RANK, kv_out[:, :RANK]), (2 * RANK, kv_out[:, RANK:])))
        base_q = jnp.dot(normed_block, w_query, preferred_element_type=jnp.float32)
        base_k = jnp.dot(normed_block, w_key, preferred_element_type=jnp.float32)
        base_v = jnp.dot(normed_block, w_value, preferred_element_type=jnp.float32)
        query_lin = (base_q + delta_q.astype(jnp.float32)).reshape(count_rows, HEADS, HEAD_WIDTH)
        queries = rotate(query_lin, offset_block).reshape(count_rows, D).astype(jnp.bfloat16)
        key_lin = (base_k + delta_k.astype(jnp.float32)).reshape(count_rows, KV_HEADS, HEAD_WIDTH)
        key_rows = rotate(key_lin, offset_block).reshape(count_rows, KVW).astype(jnp.bfloat16)
        value_rows = (base_v + delta_v.astype(jnp.float32)).astype(jnp.bfloat16)
        return (queries, jnp.concatenate([key_rows, value_rows], axis=1))
    queries, key_value = lax.map(project, (normed.reshape(blocks, TOK_DEV, D), slot_of.reshape(blocks, TOK_DEV), offset.reshape(blocks, TOK_DEV)))
    queries = queries.reshape(TOKENS, D)
    key_value = key_value.reshape(TOKENS, 2 * KVW)
    key_span = REACH * TOK_DEV
    padded_kv = jnp.concatenate([jnp.zeros((key_span, 2 * KVW), jnp.bfloat16), key_value], axis=0)
    key_positions = jnp.arange(TOKENS + key_span, dtype=jnp.int32) - key_span
    key_segment = prompt_index(key_positions, lengths)[0]

    def attend_block(block_index):
        first_row = (block_index * TOK_DEV).astype(jnp.int32)
        window = lax.dynamic_slice_in_dim(padded_kv, first_row, key_span + TOK_DEV, 0)
        window_segment = lax.dynamic_slice_in_dim(key_segment, first_row, key_span + TOK_DEV, 0)
        window_position = lax.dynamic_slice_in_dim(key_positions, first_row, key_span + TOK_DEV, 0)
        query_block = lax.dynamic_slice_in_dim(queries, first_row, TOK_DEV, 0)
        query_segment = lax.dynamic_slice_in_dim(segment, first_row, TOK_DEV, 0)
        query_position = lax.dynamic_slice_in_dim(positions, first_row, TOK_DEV, 0)
        allowed = (query_segment[:, None] == window_segment[None, :]) & (window_position[None, :] <= query_position[:, None])
        return attend(query_block, window, allowed)
    attended = lax.map(attend_block, jnp.arange(blocks, dtype=jnp.int32))

    def finish(inputs):
        attn_block, slot_block, token_block = inputs
        delta_o = adapter_terms(attn_block, slot_block, o_in, ((0, o_out),))[0]
        projected_out = jnp.dot(attn_block, w_output, preferred_element_type=jnp.float32) + delta_o.astype(jnp.float32)
        return (token_block.astype(jnp.float32) + projected_out).astype(jnp.bfloat16)
    mixed_rows = lax.map(finish, (attended, slot_of.reshape(blocks, TOK_DEV), tokens.reshape(blocks, TOK_DEV, D)))
    return (mixed_rows.reshape(TOKENS, D), key_value)
```

```python
import math

import jax
import jax.numpy as jnp
from jax import lax
from jax.sharding import PartitionSpec as P

D = 1152
HEADS = 18
KV_HEADS = 6
HEAD_WIDTH = 64
RANK = 16
REACH = 12
KVW = 384
SEG_DEV = 5


EPS = 1e-05
THETA = 10000.0


def from_behind(block, axis, distance):
    devices = range(lax.axis_size(axis))
    route = [(i - distance, i) for i in devices if i - distance in devices]
    return lax.ppermute(block, axis, route)


def rms_norm(row_block, gain_vec):
    widened = row_block.astype(jnp.float32)
    inverse_rms = lax.rsqrt(jnp.mean(widened * widened, axis=-1, keepdims=True) + EPS)
    return (widened * inverse_rms * gain_vec.astype(jnp.float32)).astype(jnp.bfloat16)


def prompt_index(positions, lengths):
    prompt_ends = jnp.cumsum(lengths)
    prompt_starts = prompt_ends - lengths
    inside = (positions[:, None] >= prompt_starts[None, :]).astype(jnp.int32)
    segment = jnp.sum(inside, axis=1) - 1
    members = jnp.arange(lengths.shape[0], dtype=jnp.int32)[None, :] == segment[:, None]
    offset = positions - jnp.sum(jnp.where(members, prompt_starts[None, :], 0), axis=1)
    return (segment, offset, members)


def slot_lookup(adapter, adapter_slot):
    matches = jnp.arange(adapter_slot.shape[0], dtype=jnp.int32)[None, :] == adapter[:, None]
    return jnp.sum(jnp.where(matches, adapter_slot[None, :], 0), axis=1)


def rotate(vectors, offset):
    half_dim = vectors.shape[-1] // 2
    frequency = jnp.exp(
        jnp.arange(half_dim, dtype=jnp.float32) * (-2.0 * math.log(THETA) / vectors.shape[-1])
    )
    angles = offset.astype(jnp.float32)[:, None] * frequency[None, :]
    cosine = jnp.cos(angles)[:, None, :]
    sine_table = jnp.sin(angles)[:, None, :]
    first_half = vectors[..., :half_dim]
    second_half = vectors[..., half_dim:]
    return jnp.concatenate(
        [
            first_half * cosine - second_half * sine_table,
            second_half * cosine + first_half * sine_table,
        ],
        axis=-1,
    )


def adapter_terms(row_block, code_rows, a_in, pieces):
    table_count, rank_cols, in_width = a_in.shape
    projected = lax.dot_general(
        row_block,
        a_in.reshape(table_count * rank_cols, in_width),
        (((1,), (1,)), ((), ())),
        preferred_element_type=jnp.float32,
    )
    chosen = (jnp.arange(table_count, dtype=jnp.int32)[None, :] == code_rows[:, None]).astype(
        jnp.float32
    )
    low_rank = (projected.reshape(-1, table_count, rank_cols) * chosen[:, :, None]).astype(
        jnp.bfloat16
    )
    results = []
    for col_start, b_table in pieces:
        width_rank = b_table.shape[1]
        section = low_rank[:, :, col_start : col_start + width_rank].reshape(
            -1, table_count * width_rank
        )
        results.append(
            jnp.dot(
                section,
                b_table.reshape(table_count * width_rank, b_table.shape[2]),
                preferred_element_type=jnp.float32,
            ).astype(jnp.bfloat16)
        )
    return tuple(results)


def on_device(
    tokens,
    norm_gain,
    w_query,
    w_key,
    w_value,
    w_output,
    qkv_in,
    q_out,
    kv_out,
    o_in,
    o_out,
    lengths,
    prompt_adapter,
    adapter_slot,
):
    tok_rows = tokens.shape[0]
    tok_count = lax.axis_size("tok")
    own_count = lax.axis_size("own")
    per_owner = qkv_in.shape[0]
    device_here = lax.axis_index(("tok", "own"))
    positions = device_here * tok_rows + jnp.arange(tok_rows, dtype=jnp.int32)
    segment, offset, members = prompt_index(positions, lengths)
    prompt_count = lengths.shape[0]
    first_segment = segment[0]
    code_rows = segment - first_segment
    normed = rms_norm(tokens, norm_gain)
    tables = (qkv_in, q_out, kv_out, o_in, o_out)
    table_shapes = tuple((table.shape[1:] for table in tables))
    packed = jnp.concatenate([table.reshape(per_owner, -1) for table in tables], axis=1)
    all_slots = lax.all_gather(packed, "own", axis=0, tiled=True)
    own_here = lax.axis_index("own")
    group_blocks = jnp.arange(tok_count, dtype=jnp.int32) * own_count + own_here
    prompt_starts = jnp.cumsum(lengths) - lengths
    group_first = (
        jnp.sum(
            (group_blocks[:, None] * tok_rows >= prompt_starts[None, :]).astype(jnp.int32), axis=1
        )
        - 1
    )
    group_segments = jnp.minimum(
        group_first[:, None] + jnp.arange(SEG_DEV, dtype=jnp.int32)[None, :], prompt_count - 1
    )
    group_slots = jnp.take(adapter_slot, jnp.take(prompt_adapter, group_segments))
    outgoing = jnp.take(all_slots, group_slots.reshape(-1), axis=0).reshape(
        tok_count, SEG_DEV, packed.shape[1]
    )
    incoming = lax.all_to_all(outgoing, "tok", 0, 0, tiled=True)
    selected = []
    col = 0
    for table_shape in table_shapes:
        width = table_shape[0] * table_shape[1]
        piece = incoming[:, :, col : col + width].reshape(
            tok_count, SEG_DEV, table_shape[0], table_shape[1]
        )
        col += width
        selected.append(
            jnp.transpose(piece, (1, 2, 0, 3)).reshape(
                SEG_DEV, table_shape[0], tok_count * table_shape[1]
            )
        )
    input_maps, query_maps, keyvalue_maps, output_in_maps, output_out_maps = selected
    delta_q, delta_k, delta_v = adapter_terms(
        normed,
        code_rows,
        input_maps,
        ((0, query_maps), (RANK, keyvalue_maps[:, :RANK]), (2 * RANK, keyvalue_maps[:, RANK:])),
    )
    base_q = jnp.dot(normed, w_query, preferred_element_type=jnp.float32)
    base_k = jnp.dot(normed, w_key, preferred_element_type=jnp.float32)
    base_v = jnp.dot(normed, w_value, preferred_element_type=jnp.float32)
    query_lin = (base_q + delta_q.astype(jnp.float32)).reshape(tok_rows, HEADS, HEAD_WIDTH)
    queries = rotate(query_lin, offset).reshape(tok_rows, D).astype(jnp.bfloat16)
    key_lin = (base_k + delta_k.astype(jnp.float32)).reshape(tok_rows, KV_HEADS, HEAD_WIDTH)
    key_rows = rotate(key_lin, offset).reshape(tok_rows, KVW).astype(jnp.bfloat16)
    value_rows = (base_v + delta_v.astype(jnp.float32)).astype(jnp.bfloat16)
    key_value = jnp.concatenate([key_rows, value_rows], axis=1)
    key_store = jnp.zeros(((REACH + 1) * tok_rows, 2 * KVW), jnp.bfloat16)
    key_store = lax.dynamic_update_slice_in_dim(key_store, key_value, REACH * tok_rows, 0)

    window = key_store
    moving = key_value
    for turn_index in range(REACH):
        moving = from_behind(moving, ("tok", "own"), 1)
        window = lax.dynamic_update_slice_in_dim(
            window, moving, (REACH - 1 - turn_index) * tok_rows, 0
        )
    key_positions = (
        device_here * tok_rows
        - REACH * tok_rows
        + jnp.arange((REACH + 1) * tok_rows, dtype=jnp.int32)
    )
    key_segment = prompt_index(key_positions, lengths)[0]
    allowed = (segment[:, None] == key_segment[None, :]) & (
        key_positions[None, :] <= positions[:, None]
    )
    groups = HEADS // KV_HEADS
    key_count = window.shape[0]
    query_head_rows = queries.reshape(tok_rows, KV_HEADS, groups, HEAD_WIDTH)
    key_head_rows = window[:, :KVW].reshape(key_count, KV_HEADS, HEAD_WIDTH)
    value_head_rows = window[:, KVW:].reshape(key_count, KV_HEADS, HEAD_WIDTH)
    score_matrix = jnp.einsum(
        "qkzr,ckr->kzqc", query_head_rows, key_head_rows, preferred_element_type=jnp.float32
    ) * HEAD_WIDTH ** (-0.5)
    score_matrix = jnp.where(allowed[None, None], score_matrix, -1e30)
    top_score = jnp.max(score_matrix, axis=-1, keepdims=True)
    exp_scores = jnp.exp(score_matrix - top_score)
    row_total = jnp.sum(exp_scores, axis=-1)
    rounded_values = exp_scores.astype(jnp.bfloat16)
    summed_rows = jnp.einsum(
        "iyxv,vip->xiyp", rounded_values, value_head_rows, preferred_element_type=jnp.float32
    )
    attn_rows = (
        (summed_rows / jnp.transpose(row_total, (2, 0, 1))[..., None])
        .reshape(tok_rows, D)
        .astype(jnp.bfloat16)
    )
    delta_o = adapter_terms(attn_rows, code_rows, output_in_maps, ((0, output_out_maps),))[0]
    projected_out = jnp.dot(
        attn_rows, w_output, preferred_element_type=jnp.float32
    ) + delta_o.astype(jnp.float32)
    mixed_rows = (tokens.astype(jnp.float32) + projected_out).astype(jnp.bfloat16)
    return (mixed_rows, key_value)


def solution(mesh):
    return jax.shard_map(
        on_device,
        mesh=mesh,
        in_specs=(
            P(("tok", "own"), None),
            P(),
            P(),
            P(),
            P(),
            P(),
            P("own", None, "tok"),
            P("own", None, "tok"),
            P("own", None, "tok"),
            P("own", None, "tok"),
            P("own", None, "tok"),
            P(),
            P(),
            P(),
        ),
        out_specs=(P(("tok", "own"), None), P(("tok", "own"), None)),
        check_vma=False,
    )
```

```python
import math

import jax
import jax.numpy as jnp
from jax import lax
from jax.sharding import PartitionSpec as P

D = 1152
HEADS = 18
KV_HEADS = 6
HEAD_WIDTH = 64
RANK = 16
REACH = 12
KVW = 384
SEG_DEV = 5


EPS = 1e-05
THETA = 10000.0


def from_behind(block, axis, distance):
    devices = range(lax.axis_size(axis))
    route = [(i - distance, i) for i in devices if i - distance in devices]
    return lax.ppermute(block, axis, route)


def rms_norm(row_block, gain_vec):
    widened = row_block.astype(jnp.float32)
    inverse_rms = lax.rsqrt(jnp.mean(widened * widened, axis=-1, keepdims=True) + EPS)
    return (widened * inverse_rms * gain_vec.astype(jnp.float32)).astype(jnp.bfloat16)


def prompt_index(positions, lengths):
    prompt_ends = jnp.cumsum(lengths)
    prompt_starts = prompt_ends - lengths
    inside = (positions[:, None] >= prompt_starts[None, :]).astype(jnp.int32)
    segment = jnp.sum(inside, axis=1) - 1
    members = jnp.arange(lengths.shape[0], dtype=jnp.int32)[None, :] == segment[:, None]
    offset = positions - jnp.sum(jnp.where(members, prompt_starts[None, :], 0), axis=1)
    return (segment, offset, members)


def slot_lookup(adapter, adapter_slot):
    matches = jnp.arange(adapter_slot.shape[0], dtype=jnp.int32)[None, :] == adapter[:, None]
    return jnp.sum(jnp.where(matches, adapter_slot[None, :], 0), axis=1)


def rotate(vectors, offset):
    half_dim = vectors.shape[-1] // 2
    frequency = jnp.exp(
        jnp.arange(half_dim, dtype=jnp.float32) * (-2.0 * math.log(THETA) / vectors.shape[-1])
    )
    angles = offset.astype(jnp.float32)[:, None] * frequency[None, :]
    cosine = jnp.cos(angles)[:, None, :]
    sine_table = jnp.sin(angles)[:, None, :]
    first_half = vectors[..., :half_dim]
    second_half = vectors[..., half_dim:]
    return jnp.concatenate(
        [
            first_half * cosine - second_half * sine_table,
            second_half * cosine + first_half * sine_table,
        ],
        axis=-1,
    )


def adapter_terms(row_block, code_rows, a_in, pieces):
    table_count, rank_cols, in_width = a_in.shape
    projected = lax.dot_general(
        row_block,
        a_in.reshape(table_count * rank_cols, in_width),
        (((1,), (1,)), ((), ())),
        preferred_element_type=jnp.float32,
    )
    chosen = (jnp.arange(table_count, dtype=jnp.int32)[None, :] == code_rows[:, None]).astype(
        jnp.float32
    )
    low_rank = (projected.reshape(-1, table_count, rank_cols) * chosen[:, :, None]).astype(
        jnp.bfloat16
    )
    results = []
    for col_start, b_table in pieces:
        width_rank = b_table.shape[1]
        section = low_rank[:, :, col_start : col_start + width_rank].reshape(
            -1, table_count * width_rank
        )
        results.append(
            jnp.dot(
                section,
                b_table.reshape(table_count * width_rank, b_table.shape[2]),
                preferred_element_type=jnp.float32,
            ).astype(jnp.bfloat16)
        )
    return tuple(results)


def on_device(
    tokens,
    norm_gain,
    w_query,
    w_key,
    w_value,
    w_output,
    qkv_in,
    q_out,
    kv_out,
    o_in,
    o_out,
    lengths,
    prompt_adapter,
    adapter_slot,
):
    tok_rows = tokens.shape[0]
    tok_count = lax.axis_size("tok")
    own_count = lax.axis_size("own")
    per_owner = qkv_in.shape[0]
    device_here = lax.axis_index(("tok", "own"))
    positions = device_here * tok_rows + jnp.arange(tok_rows, dtype=jnp.int32)
    segment, offset, members = prompt_index(positions, lengths)
    prompt_count = lengths.shape[0]
    first_segment = segment[0]
    code_rows = segment - first_segment
    normed = rms_norm(tokens, norm_gain)
    tables = (qkv_in, q_out, kv_out, o_in, o_out)
    table_shapes = tuple((table.shape[1:] for table in tables))
    packed = jnp.concatenate([table.reshape(per_owner, -1) for table in tables], axis=1)
    all_slots = lax.all_gather(packed, "own", axis=0, tiled=True)
    own_here = lax.axis_index("own")
    group_blocks = jnp.arange(tok_count, dtype=jnp.int32) * own_count + own_here
    prompt_starts = jnp.cumsum(lengths) - lengths
    group_first = (
        jnp.sum(
            (group_blocks[:, None] * tok_rows >= prompt_starts[None, :]).astype(jnp.int32), axis=1
        )
        - 1
    )
    group_segments = jnp.minimum(
        group_first[:, None] + jnp.arange(SEG_DEV, dtype=jnp.int32)[None, :], prompt_count - 1
    )
    group_slots = jnp.take(adapter_slot, jnp.take(prompt_adapter, group_segments))
    outgoing = jnp.take(all_slots, group_slots.reshape(-1), axis=0).reshape(
        tok_count, SEG_DEV, packed.shape[1]
    )
    split_col = sum(shape[0] * shape[1] for shape in table_shapes[:3])
    incoming = jnp.concatenate(
        [
            lax.all_to_all(outgoing[:, :, :split_col], "tok", 0, 0, tiled=True),
            lax.all_to_all(outgoing[:, :, split_col:], "tok", 0, 0, tiled=True),
        ],
        axis=2,
    )
    selected = []
    col = 0
    for table_shape in table_shapes:
        width = table_shape[0] * table_shape[1]
        piece = incoming[:, :, col : col + width].reshape(
            tok_count, SEG_DEV, table_shape[0], table_shape[1]
        )
        col += width
        selected.append(
            jnp.transpose(piece, (1, 2, 0, 3)).reshape(
                SEG_DEV, table_shape[0], tok_count * table_shape[1]
            )
        )
    input_maps, query_maps, keyvalue_maps, output_in_maps, output_out_maps = selected
    delta_q, delta_k, delta_v = adapter_terms(
        normed,
        code_rows,
        input_maps,
        ((0, query_maps), (RANK, keyvalue_maps[:, :RANK]), (2 * RANK, keyvalue_maps[:, RANK:])),
    )
    base_q = jnp.dot(normed, w_query, preferred_element_type=jnp.float32)
    base_k = jnp.dot(normed, w_key, preferred_element_type=jnp.float32)
    base_v = jnp.dot(normed, w_value, preferred_element_type=jnp.float32)
    query_lin = (base_q + delta_q.astype(jnp.float32)).reshape(tok_rows, HEADS, HEAD_WIDTH)
    queries = rotate(query_lin, offset).reshape(tok_rows, D).astype(jnp.bfloat16)
    key_lin = (base_k + delta_k.astype(jnp.float32)).reshape(tok_rows, KV_HEADS, HEAD_WIDTH)
    key_rows = rotate(key_lin, offset).reshape(tok_rows, KVW).astype(jnp.bfloat16)
    value_rows = (base_v + delta_v.astype(jnp.float32)).astype(jnp.bfloat16)
    key_value = jnp.concatenate([key_rows, value_rows], axis=1)

    earlier = [from_behind(key_value, ("tok", "own"), distance) for distance in range(REACH, 0, -1)]
    window = jnp.concatenate(earlier + [key_value], axis=0)
    key_positions = (
        device_here * tok_rows
        - REACH * tok_rows
        + jnp.arange((REACH + 1) * tok_rows, dtype=jnp.int32)
    )
    key_segment = prompt_index(key_positions, lengths)[0]
    allowed = (segment[:, None] == key_segment[None, :]) & (
        key_positions[None, :] <= positions[:, None]
    )
    groups = HEADS // KV_HEADS
    key_count = window.shape[0]
    query_head_rows = queries.reshape(tok_rows, KV_HEADS, groups, HEAD_WIDTH)
    key_head_rows = window[:, :KVW].reshape(key_count, KV_HEADS, HEAD_WIDTH)
    value_head_rows = window[:, KVW:].reshape(key_count, KV_HEADS, HEAD_WIDTH)
    score_matrix = jnp.einsum(
        "qkzr,ckr->kzqc", query_head_rows, key_head_rows, preferred_element_type=jnp.float32
    ) * HEAD_WIDTH ** (-0.5)
    score_matrix = jnp.where(allowed[None, None], score_matrix, -1e30)
    top_score = jnp.max(score_matrix, axis=-1, keepdims=True)
    exp_scores = jnp.exp(score_matrix - top_score)
    row_total = jnp.sum(exp_scores, axis=-1)
    rounded_values = exp_scores.astype(jnp.bfloat16)
    summed_rows = jnp.einsum(
        "iyxv,vip->xiyp", rounded_values, value_head_rows, preferred_element_type=jnp.float32
    )
    attn_rows = (
        (summed_rows / jnp.transpose(row_total, (2, 0, 1))[..., None])
        .reshape(tok_rows, D)
        .astype(jnp.bfloat16)
    )
    delta_o = adapter_terms(attn_rows, code_rows, output_in_maps, ((0, output_out_maps),))[0]
    projected_out = jnp.dot(
        attn_rows, w_output, preferred_element_type=jnp.float32
    ) + delta_o.astype(jnp.float32)
    mixed_rows = (tokens.astype(jnp.float32) + projected_out).astype(jnp.bfloat16)
    return (mixed_rows, key_value)


def solution(mesh):
    return jax.shard_map(
        on_device,
        mesh=mesh,
        in_specs=(
            P(("tok", "own"), None),
            P(),
            P(),
            P(),
            P(),
            P(),
            P("own", None, "tok"),
            P("own", None, "tok"),
            P("own", None, "tok"),
            P("own", None, "tok"),
            P("own", None, "tok"),
            P(),
            P(),
            P(),
        ),
        out_specs=(P(("tok", "own"), None), P(("tok", "own"), None)),
        check_vma=False,
    )
```

```python
import math

import jax
import jax.numpy as jnp
from jax import lax
from jax.sharding import PartitionSpec as P

D = 1152
HEADS = 18
KV_HEADS = 6
HEAD_WIDTH = 64
RANK = 16
REACH = 12
KVW = 384
SEG_DEV = 5


EPS = 1e-05
THETA = 10000.0


def from_behind(block, axis, distance):
    devices = range(lax.axis_size(axis))
    route = [(i - distance, i) for i in devices if i - distance in devices]
    return lax.ppermute(block, axis, route)


def rms_norm(row_block, gain_vec):
    widened = row_block.astype(jnp.float32)
    inverse_rms = lax.rsqrt(jnp.mean(widened * widened, axis=-1, keepdims=True) + EPS)
    return (widened * inverse_rms * gain_vec.astype(jnp.float32)).astype(jnp.bfloat16)


def prompt_index(positions, lengths):
    prompt_ends = jnp.cumsum(lengths)
    prompt_starts = prompt_ends - lengths
    inside = (positions[:, None] >= prompt_starts[None, :]).astype(jnp.int32)
    segment = jnp.sum(inside, axis=1) - 1
    members = jnp.arange(lengths.shape[0], dtype=jnp.int32)[None, :] == segment[:, None]
    offset = positions - jnp.sum(jnp.where(members, prompt_starts[None, :], 0), axis=1)
    return (segment, offset, members)


def slot_lookup(adapter, adapter_slot):
    matches = jnp.arange(adapter_slot.shape[0], dtype=jnp.int32)[None, :] == adapter[:, None]
    return jnp.sum(jnp.where(matches, adapter_slot[None, :], 0), axis=1)


def rotate(vectors, offset):
    half_dim = vectors.shape[-1] // 2
    frequency = jnp.exp(
        jnp.arange(half_dim, dtype=jnp.float32) * (-2.0 * math.log(THETA) / vectors.shape[-1])
    )
    angles = offset.astype(jnp.float32)[:, None] * frequency[None, :]
    cosine = jnp.cos(angles)[:, None, :]
    sine_table = jnp.sin(angles)[:, None, :]
    first_half = vectors[..., :half_dim]
    second_half = vectors[..., half_dim:]
    return jnp.concatenate(
        [
            first_half * cosine - second_half * sine_table,
            second_half * cosine + first_half * sine_table,
        ],
        axis=-1,
    )


def adapter_terms(row_block, code_rows, a_in, pieces):
    table_count, rank_cols, in_width = a_in.shape
    projected = lax.dot_general(
        row_block,
        a_in.reshape(table_count * rank_cols, in_width),
        (((1,), (1,)), ((), ())),
        preferred_element_type=jnp.float32,
    )
    chosen = (jnp.arange(table_count, dtype=jnp.int32)[None, :] == code_rows[:, None]).astype(
        jnp.float32
    )
    low_rank = (projected.reshape(-1, table_count, rank_cols) * chosen[:, :, None]).astype(
        jnp.bfloat16
    )
    results = []
    for col_start, b_table in pieces:
        width_rank = b_table.shape[1]
        section = low_rank[:, :, col_start : col_start + width_rank].reshape(
            -1, table_count * width_rank
        )
        results.append(
            jnp.dot(
                section,
                b_table.reshape(table_count * width_rank, b_table.shape[2]),
                preferred_element_type=jnp.float32,
            ).astype(jnp.bfloat16)
        )
    return tuple(results)


def on_device(
    tokens,
    norm_gain,
    w_query,
    w_key,
    w_value,
    w_output,
    qkv_in,
    q_out,
    kv_out,
    o_in,
    o_out,
    lengths,
    prompt_adapter,
    adapter_slot,
):
    tok_rows = tokens.shape[0]
    tok_count = lax.axis_size("tok")
    own_count = lax.axis_size("own")
    per_owner = qkv_in.shape[0]
    device_here = lax.axis_index(("tok", "own"))
    positions = device_here * tok_rows + jnp.arange(tok_rows, dtype=jnp.int32)
    segment, offset, members = prompt_index(positions, lengths)
    prompt_count = lengths.shape[0]
    first_segment = segment[0]
    code_rows = segment - first_segment
    normed = rms_norm(tokens, norm_gain)
    tables = (qkv_in, q_out, kv_out, o_in, o_out)
    table_shapes = tuple((table.shape[1:] for table in tables))
    packed = jnp.concatenate([table.reshape(per_owner, -1) for table in tables], axis=1)
    all_slots = lax.all_gather(packed, "own", axis=0, tiled=True)
    own_here = lax.axis_index("own")
    group_blocks = jnp.arange(tok_count, dtype=jnp.int32) * own_count + own_here
    prompt_starts = jnp.cumsum(lengths) - lengths
    group_first = (
        jnp.sum(
            (group_blocks[:, None] * tok_rows >= prompt_starts[None, :]).astype(jnp.int32), axis=1
        )
        - 1
    )
    group_segments = jnp.minimum(
        group_first[:, None] + jnp.arange(SEG_DEV, dtype=jnp.int32)[None, :], prompt_count - 1
    )
    group_slots = jnp.take(adapter_slot, jnp.take(prompt_adapter, group_segments))
    outgoing = jnp.take(all_slots, group_slots.reshape(-1), axis=0).reshape(
        tok_count, SEG_DEV, packed.shape[1]
    )
    split_col = sum(shape[0] * shape[1] for shape in table_shapes[:3])
    incoming_first = lax.all_to_all(outgoing[:, :, :split_col], "tok", 0, 0, tiled=True)
    incoming_first, outgoing_later = lax.optimization_barrier(
        (incoming_first, outgoing[:, :, split_col:])
    )
    incoming = jnp.concatenate(
        [incoming_first, lax.all_to_all(outgoing_later, "tok", 0, 0, tiled=True)], axis=2
    )
    selected = []
    col = 0
    for table_shape in table_shapes:
        width = table_shape[0] * table_shape[1]
        piece = incoming[:, :, col : col + width].reshape(
            tok_count, SEG_DEV, table_shape[0], table_shape[1]
        )
        col += width
        selected.append(
            jnp.transpose(piece, (1, 2, 0, 3)).reshape(
                SEG_DEV, table_shape[0], tok_count * table_shape[1]
            )
        )
    input_maps, query_maps, keyvalue_maps, output_in_maps, output_out_maps = selected
    delta_q, delta_k, delta_v = adapter_terms(
        normed,
        code_rows,
        input_maps,
        ((0, query_maps), (RANK, keyvalue_maps[:, :RANK]), (2 * RANK, keyvalue_maps[:, RANK:])),
    )
    base_q = jnp.dot(normed, w_query, preferred_element_type=jnp.float32)
    base_k = jnp.dot(normed, w_key, preferred_element_type=jnp.float32)
    base_v = jnp.dot(normed, w_value, preferred_element_type=jnp.float32)
    query_lin = (base_q + delta_q.astype(jnp.float32)).reshape(tok_rows, HEADS, HEAD_WIDTH)
    queries = rotate(query_lin, offset).reshape(tok_rows, D).astype(jnp.bfloat16)
    key_lin = (base_k + delta_k.astype(jnp.float32)).reshape(tok_rows, KV_HEADS, HEAD_WIDTH)
    key_rows = rotate(key_lin, offset).reshape(tok_rows, KVW).astype(jnp.bfloat16)
    value_rows = (base_v + delta_v.astype(jnp.float32)).astype(jnp.bfloat16)
    key_value = jnp.concatenate([key_rows, value_rows], axis=1)

    earlier = [from_behind(key_value, ("tok", "own"), distance) for distance in range(REACH, 0, -1)]
    window = jnp.concatenate(earlier + [key_value], axis=0)
    key_positions = (
        device_here * tok_rows
        - REACH * tok_rows
        + jnp.arange((REACH + 1) * tok_rows, dtype=jnp.int32)
    )
    key_segment = prompt_index(key_positions, lengths)[0]
    allowed = (segment[:, None] == key_segment[None, :]) & (
        key_positions[None, :] <= positions[:, None]
    )
    groups = HEADS // KV_HEADS
    key_count = window.shape[0]
    query_head_rows = queries.reshape(tok_rows, KV_HEADS, groups, HEAD_WIDTH)
    key_head_rows = window[:, :KVW].reshape(key_count, KV_HEADS, HEAD_WIDTH)
    value_head_rows = window[:, KVW:].reshape(key_count, KV_HEADS, HEAD_WIDTH)
    score_matrix = jnp.einsum(
        "qkzr,ckr->kzqc", query_head_rows, key_head_rows, preferred_element_type=jnp.float32
    ) * HEAD_WIDTH ** (-0.5)
    score_matrix = jnp.where(allowed[None, None], score_matrix, -1e30)
    top_score = jnp.max(score_matrix, axis=-1, keepdims=True)
    exp_scores = jnp.exp(score_matrix - top_score)
    row_total = jnp.sum(exp_scores, axis=-1)
    rounded_values = exp_scores.astype(jnp.bfloat16)
    summed_rows = jnp.einsum(
        "iyxv,vip->xiyp", rounded_values, value_head_rows, preferred_element_type=jnp.float32
    )
    attn_rows = (
        (summed_rows / jnp.transpose(row_total, (2, 0, 1))[..., None])
        .reshape(tok_rows, D)
        .astype(jnp.bfloat16)
    )
    delta_o = adapter_terms(attn_rows, code_rows, output_in_maps, ((0, output_out_maps),))[0]
    projected_out = jnp.dot(
        attn_rows, w_output, preferred_element_type=jnp.float32
    ) + delta_o.astype(jnp.float32)
    mixed_rows = (tokens.astype(jnp.float32) + projected_out).astype(jnp.bfloat16)
    return (mixed_rows, key_value)


def solution(mesh):
    return jax.shard_map(
        on_device,
        mesh=mesh,
        in_specs=(
            P(("tok", "own"), None),
            P(),
            P(),
            P(),
            P(),
            P(),
            P("own", None, "tok"),
            P("own", None, "tok"),
            P("own", None, "tok"),
            P("own", None, "tok"),
            P("own", None, "tok"),
            P(),
            P(),
            P(),
        ),
        out_specs=(P(("tok", "own"), None), P(("tok", "own"), None)),
        check_vma=False,
    )
```

```python
import math

import functools

import jax
import jax.numpy as jnp
from jax import lax
from jax.experimental import pallas as pl
from jax.experimental.pallas import tpu as pltpu
from jax.sharding import PartitionSpec as P

D = 1152
HEADS = 18
KV_HEADS = 6
HEAD_WIDTH = 64
RANK = 16
REACH = 12
KVW = 384
SEG_DEV = 5


EPS = 1e-05
THETA = 10000.0


def from_behind(block, axis, distance):
    devices = range(lax.axis_size(axis))
    route = [(i - distance, i) for i in devices if i - distance in devices]
    return lax.ppermute(block, axis, route)


def rms_norm(row_block, gain_vec):
    widened = row_block.astype(jnp.float32)
    inverse_rms = lax.rsqrt(jnp.mean(widened * widened, axis=-1, keepdims=True) + EPS)
    return (widened * inverse_rms * gain_vec.astype(jnp.float32)).astype(jnp.bfloat16)


def prompt_index(positions, lengths):
    prompt_ends = jnp.cumsum(lengths)
    prompt_starts = prompt_ends - lengths
    inside = (positions[:, None] >= prompt_starts[None, :]).astype(jnp.int32)
    segment = jnp.sum(inside, axis=1) - 1
    members = jnp.arange(lengths.shape[0], dtype=jnp.int32)[None, :] == segment[:, None]
    offset = positions - jnp.sum(jnp.where(members, prompt_starts[None, :], 0), axis=1)
    return (segment, offset, members)


def slot_lookup(adapter, adapter_slot):
    matches = jnp.arange(adapter_slot.shape[0], dtype=jnp.int32)[None, :] == adapter[:, None]
    return jnp.sum(jnp.where(matches, adapter_slot[None, :], 0), axis=1)


def rotate(vectors, offset):
    half_dim = vectors.shape[-1] // 2
    frequency = jnp.exp(
        jnp.arange(half_dim, dtype=jnp.float32) * (-2.0 * math.log(THETA) / vectors.shape[-1])
    )
    angles = offset.astype(jnp.float32)[:, None] * frequency[None, :]
    cosine = jnp.cos(angles)[:, None, :]
    sine_table = jnp.sin(angles)[:, None, :]
    first_half = vectors[..., :half_dim]
    second_half = vectors[..., half_dim:]
    return jnp.concatenate(
        [
            first_half * cosine - second_half * sine_table,
            second_half * cosine + first_half * sine_table,
        ],
        axis=-1,
    )


def adapter_terms(row_block, code_rows, a_in, pieces):
    table_count, rank_cols, in_width = a_in.shape
    projected = lax.dot_general(
        row_block,
        a_in.reshape(table_count * rank_cols, in_width),
        (((1,), (1,)), ((), ())),
        preferred_element_type=jnp.float32,
    )
    chosen = (jnp.arange(table_count, dtype=jnp.int32)[None, :] == code_rows[:, None]).astype(
        jnp.float32
    )
    low_rank = (projected.reshape(-1, table_count, rank_cols) * chosen[:, :, None]).astype(
        jnp.bfloat16
    )
    results = []
    for col_start, b_table in pieces:
        width_rank = b_table.shape[1]
        section = low_rank[:, :, col_start : col_start + width_rank].reshape(
            -1, table_count * width_rank
        )
        results.append(
            jnp.dot(
                section,
                b_table.reshape(table_count * width_rank, b_table.shape[2]),
                preferred_element_type=jnp.float32,
            ).astype(jnp.bfloat16)
        )
    return tuple(results)


def attention_kernel(block_count, query_ref, *refs):
    value_refs = refs[:block_count]
    query_segment_ref, key_segment_ref, out_ref, score_ref = refs[block_count:]
    rows = query_ref.shape[0]
    groups = HEADS // KV_HEADS
    query_segment = query_segment_ref[...]
    row_index = lax.broadcasted_iota(jnp.int32, (rows, rows), 0)
    col_index = lax.broadcasted_iota(jnp.int32, (rows, rows), 1)
    masks = []
    for block in range(block_count):
        same = query_segment == key_segment_ref[:, block * rows : (block + 1) * rows]
        if block == block_count - 1:
            same = same & (col_index <= row_index)
        masks.append(same)
    for kv_head in range(KV_HEADS):
        key_cols = slice(kv_head * HEAD_WIDTH, (kv_head + 1) * HEAD_WIDTH)
        value_cols = slice(KVW + kv_head * HEAD_WIDTH, KVW + (kv_head + 1) * HEAD_WIDTH)
        for group in range(groups):
            head = kv_head * groups + group
            head_cols = slice(head * HEAD_WIDTH, (head + 1) * HEAD_WIDTH)
            query_head = query_ref[:, head_cols]
            for block in range(block_count):
                score = lax.dot_general(
                    query_head,
                    value_refs[block][:, key_cols],
                    (((1,), (1,)), ((), ())),
                    preferred_element_type=jnp.float32,
                ) * HEAD_WIDTH ** (-0.5)
                score_ref[:, block * rows : (block + 1) * rows] = jnp.where(
                    masks[block], score, -1e30
                )
            scores = score_ref[...]
            top_score = jnp.max(scores, axis=1, keepdims=True)
            exp_scores = jnp.exp(scores - top_score)
            row_total = jnp.sum(exp_scores, axis=1, keepdims=True)
            rounded = exp_scores.astype(jnp.bfloat16)
            summed = jnp.zeros((rows, HEAD_WIDTH), jnp.float32)
            for block in range(block_count):
                summed = summed + jnp.dot(
                    rounded[:, block * rows : (block + 1) * rows],
                    value_refs[block][:, value_cols],
                    preferred_element_type=jnp.float32,
                )
            out_ref[:, head_cols] = (summed / row_total).astype(out_ref.dtype)


def attend_blocks(queries, blocks, query_segment, key_segment):
    rows = queries.shape[0]
    block_count = len(blocks)
    keys = block_count * rows
    vmem = pl.BlockSpec(memory_space=pltpu.VMEM)
    return pl.pallas_call(
        functools.partial(attention_kernel, block_count),
        out_shape=jax.ShapeDtypeStruct(queries.shape, jnp.bfloat16),
        in_specs=[vmem] * (block_count + 3),
        out_specs=vmem,
        scratch_shapes=[pltpu.VMEM((rows, keys), jnp.float32)],
        cost_estimate=pl.CostEstimate(
            flops=4 * HEADS * rows * keys * HEAD_WIDTH,
            transcendentals=HEADS * rows * keys,
            bytes_accessed=2 * (2 * queries.size + block_count * blocks[0].size),
        ),
    )(queries, *blocks, query_segment.reshape(rows, 1), key_segment.reshape(1, keys))


def on_device(
    tokens,
    norm_gain,
    w_query,
    w_key,
    w_value,
    w_output,
    qkv_in,
    q_out,
    kv_out,
    o_in,
    o_out,
    lengths,
    prompt_adapter,
    adapter_slot,
):
    tok_rows = tokens.shape[0]
    tok_count = lax.axis_size("tok")
    own_count = lax.axis_size("own")
    per_owner = qkv_in.shape[0]
    device_here = lax.axis_index(("tok", "own"))
    positions = device_here * tok_rows + jnp.arange(tok_rows, dtype=jnp.int32)
    segment, offset, members = prompt_index(positions, lengths)
    prompt_count = lengths.shape[0]
    first_segment = segment[0]
    code_rows = segment - first_segment
    normed = rms_norm(tokens, norm_gain)
    tables = (qkv_in, q_out, kv_out, o_in, o_out)
    table_shapes = tuple((table.shape[1:] for table in tables))
    packed = jnp.concatenate([table.reshape(per_owner, -1) for table in tables], axis=1)
    all_slots = lax.all_gather(packed, "own", axis=0, tiled=True)
    own_here = lax.axis_index("own")
    group_blocks = jnp.arange(tok_count, dtype=jnp.int32) * own_count + own_here
    prompt_starts = jnp.cumsum(lengths) - lengths
    group_first = (
        jnp.sum(
            (group_blocks[:, None] * tok_rows >= prompt_starts[None, :]).astype(jnp.int32), axis=1
        )
        - 1
    )
    group_segments = jnp.minimum(
        group_first[:, None] + jnp.arange(SEG_DEV, dtype=jnp.int32)[None, :], prompt_count - 1
    )
    group_slots = jnp.take(adapter_slot, jnp.take(prompt_adapter, group_segments))
    outgoing = jnp.take(all_slots, group_slots.reshape(-1), axis=0).reshape(
        tok_count, SEG_DEV, packed.shape[1]
    )
    split_col = sum(shape[0] * shape[1] for shape in table_shapes[:3])
    incoming = jnp.concatenate(
        [
            lax.all_to_all(outgoing[:, :, :split_col], "tok", 0, 0, tiled=True),
            lax.all_to_all(outgoing[:, :, split_col:], "tok", 0, 0, tiled=True),
        ],
        axis=2,
    )
    selected = []
    col = 0
    for table_shape in table_shapes:
        width = table_shape[0] * table_shape[1]
        piece = incoming[:, :, col : col + width].reshape(
            tok_count, SEG_DEV, table_shape[0], table_shape[1]
        )
        col += width
        selected.append(
            jnp.transpose(piece, (1, 2, 0, 3)).reshape(
                SEG_DEV, table_shape[0], tok_count * table_shape[1]
            )
        )
    input_maps, query_maps, keyvalue_maps, output_in_maps, output_out_maps = selected
    delta_q, delta_k, delta_v = adapter_terms(
        normed,
        code_rows,
        input_maps,
        ((0, query_maps), (RANK, keyvalue_maps[:, :RANK]), (2 * RANK, keyvalue_maps[:, RANK:])),
    )
    base_q = jnp.dot(normed, w_query, preferred_element_type=jnp.float32)
    base_k = jnp.dot(normed, w_key, preferred_element_type=jnp.float32)
    base_v = jnp.dot(normed, w_value, preferred_element_type=jnp.float32)
    query_lin = (base_q + delta_q.astype(jnp.float32)).reshape(tok_rows, HEADS, HEAD_WIDTH)
    queries = rotate(query_lin, offset).reshape(tok_rows, D).astype(jnp.bfloat16)
    key_lin = (base_k + delta_k.astype(jnp.float32)).reshape(tok_rows, KV_HEADS, HEAD_WIDTH)
    key_rows = rotate(key_lin, offset).reshape(tok_rows, KVW).astype(jnp.bfloat16)
    value_rows = (base_v + delta_v.astype(jnp.float32)).astype(jnp.bfloat16)
    key_value = jnp.concatenate([key_rows, value_rows], axis=1)

    earlier = [from_behind(key_value, ("tok", "own"), distance) for distance in range(REACH, 0, -1)]
    key_positions = (
        device_here * tok_rows
        - REACH * tok_rows
        + jnp.arange((REACH + 1) * tok_rows, dtype=jnp.int32)
    )
    key_segment = prompt_index(key_positions, lengths)[0]
    attn_rows = attend_blocks(queries, earlier + [key_value], segment, key_segment)
    delta_o = adapter_terms(attn_rows, code_rows, output_in_maps, ((0, output_out_maps),))[0]
    projected_out = jnp.dot(
        attn_rows, w_output, preferred_element_type=jnp.float32
    ) + delta_o.astype(jnp.float32)
    mixed_rows = (tokens.astype(jnp.float32) + projected_out).astype(jnp.bfloat16)
    return (mixed_rows, key_value)


def solution(mesh):
    return jax.shard_map(
        on_device,
        mesh=mesh,
        in_specs=(
            P(("tok", "own"), None),
            P(),
            P(),
            P(),
            P(),
            P(),
            P("own", None, "tok"),
            P("own", None, "tok"),
            P("own", None, "tok"),
            P("own", None, "tok"),
            P("own", None, "tok"),
            P(),
            P(),
            P(),
        ),
        out_specs=(P(("tok", "own"), None), P(("tok", "own"), None)),
        check_vma=False,
    )
```

```python
import math

import functools

import jax
import jax.numpy as jnp
from jax import lax
from jax.experimental import pallas as pl
from jax.experimental.pallas import tpu as pltpu
from jax.sharding import PartitionSpec as P

D = 1152
HEADS = 18
KV_HEADS = 6
HEAD_WIDTH = 64
RANK = 16
REACH = 12
KVW = 384
SEG_DEV = 5


EPS = 1e-05
THETA = 10000.0


def from_behind(block, axis, distance):
    devices = range(lax.axis_size(axis))
    route = [(i - distance, i) for i in devices if i - distance in devices]
    return lax.ppermute(block, axis, route)


def rms_norm(row_block, gain_vec):
    widened = row_block.astype(jnp.float32)
    inverse_rms = lax.rsqrt(jnp.mean(widened * widened, axis=-1, keepdims=True) + EPS)
    return (widened * inverse_rms * gain_vec.astype(jnp.float32)).astype(jnp.bfloat16)


def prompt_index(positions, lengths):
    prompt_ends = jnp.cumsum(lengths)
    prompt_starts = prompt_ends - lengths
    inside = (positions[:, None] >= prompt_starts[None, :]).astype(jnp.int32)
    segment = jnp.sum(inside, axis=1) - 1
    members = jnp.arange(lengths.shape[0], dtype=jnp.int32)[None, :] == segment[:, None]
    offset = positions - jnp.sum(jnp.where(members, prompt_starts[None, :], 0), axis=1)
    return (segment, offset, members)


def slot_lookup(adapter, adapter_slot):
    matches = jnp.arange(adapter_slot.shape[0], dtype=jnp.int32)[None, :] == adapter[:, None]
    return jnp.sum(jnp.where(matches, adapter_slot[None, :], 0), axis=1)


def rotate(vectors, offset):
    half_dim = vectors.shape[-1] // 2
    frequency = jnp.exp(
        jnp.arange(half_dim, dtype=jnp.float32) * (-2.0 * math.log(THETA) / vectors.shape[-1])
    )
    angles = offset.astype(jnp.float32)[:, None] * frequency[None, :]
    cosine = jnp.cos(angles)[:, None, :]
    sine_table = jnp.sin(angles)[:, None, :]
    first_half = vectors[..., :half_dim]
    second_half = vectors[..., half_dim:]
    return jnp.concatenate(
        [
            first_half * cosine - second_half * sine_table,
            second_half * cosine + first_half * sine_table,
        ],
        axis=-1,
    )


def adapter_terms(row_block, code_rows, a_in, pieces):
    table_count, rank_cols, in_width = a_in.shape
    projected = lax.dot_general(
        row_block,
        a_in.reshape(table_count * rank_cols, in_width),
        (((1,), (1,)), ((), ())),
        preferred_element_type=jnp.float32,
    )
    chosen = (jnp.arange(table_count, dtype=jnp.int32)[None, :] == code_rows[:, None]).astype(
        jnp.float32
    )
    low_rank = (projected.reshape(-1, table_count, rank_cols) * chosen[:, :, None]).astype(
        jnp.bfloat16
    )
    results = []
    for col_start, b_table in pieces:
        width_rank = b_table.shape[1]
        section = low_rank[:, :, col_start : col_start + width_rank].reshape(
            -1, table_count * width_rank
        )
        results.append(
            jnp.dot(
                section,
                b_table.reshape(table_count * width_rank, b_table.shape[2]),
                preferred_element_type=jnp.float32,
            ).astype(jnp.bfloat16)
        )
    return tuple(results)


def attention_kernel(operand_count, query_ref, *refs):
    operand_refs = refs[:operand_count]
    query_segment_ref, key_segment_ref, out_ref, score_ref = refs[operand_count:]
    rows = query_ref.shape[0]
    value_refs = [
        operand.at[start : start + rows]
        for operand in operand_refs
        for start in range(0, operand.shape[0], rows)
    ]
    block_count = len(value_refs)
    groups = HEADS // KV_HEADS
    query_segment = query_segment_ref[...]
    row_index = lax.broadcasted_iota(jnp.int32, (rows, rows), 0)
    col_index = lax.broadcasted_iota(jnp.int32, (rows, rows), 1)
    masks = []
    for block in range(block_count):
        same = query_segment == key_segment_ref[:, block * rows : (block + 1) * rows]
        if block == block_count - 1:
            same = same & (col_index <= row_index)
        masks.append(same)
    for kv_head in range(KV_HEADS):
        key_cols = slice(kv_head * HEAD_WIDTH, (kv_head + 1) * HEAD_WIDTH)
        value_cols = slice(KVW + kv_head * HEAD_WIDTH, KVW + (kv_head + 1) * HEAD_WIDTH)
        for group in range(groups):
            head = kv_head * groups + group
            head_cols = slice(head * HEAD_WIDTH, (head + 1) * HEAD_WIDTH)
            query_head = query_ref[:, head_cols]
            for block in range(block_count):
                score = lax.dot_general(
                    query_head,
                    value_refs[block][:, key_cols],
                    (((1,), (1,)), ((), ())),
                    preferred_element_type=jnp.float32,
                ) * HEAD_WIDTH ** (-0.5)
                score_ref[:, block * rows : (block + 1) * rows] = jnp.where(
                    masks[block], score, -1e30
                )
            scores = score_ref[...]
            top_score = jnp.max(scores, axis=1, keepdims=True)
            exp_scores = jnp.exp(scores - top_score)
            row_total = jnp.sum(exp_scores, axis=1, keepdims=True)
            rounded = exp_scores.astype(jnp.bfloat16)
            summed = jnp.zeros((rows, HEAD_WIDTH), jnp.float32)
            for block in range(block_count):
                summed = summed + jnp.dot(
                    rounded[:, block * rows : (block + 1) * rows],
                    value_refs[block][:, value_cols],
                    preferred_element_type=jnp.float32,
                )
            out_ref[:, head_cols] = (summed / row_total).astype(out_ref.dtype)


def attend_blocks(queries, blocks, query_segment, key_segment):
    rows = queries.shape[0]
    block_count = len(blocks)
    keys = sum(block.shape[0] for block in blocks)
    vmem = pl.BlockSpec(memory_space=pltpu.VMEM)
    return pl.pallas_call(
        functools.partial(attention_kernel, block_count),
        out_shape=jax.ShapeDtypeStruct(queries.shape, jnp.bfloat16),
        in_specs=[vmem] * (block_count + 3),
        out_specs=vmem,
        scratch_shapes=[pltpu.VMEM((rows, keys), jnp.float32)],
        cost_estimate=pl.CostEstimate(
            flops=4 * HEADS * rows * keys * HEAD_WIDTH,
            transcendentals=HEADS * rows * keys,
            bytes_accessed=2 * (2 * queries.size + keys * blocks[0].shape[1]),
        ),
    )(queries, *blocks, query_segment.reshape(rows, 1), key_segment.reshape(1, keys))


def on_device(
    tokens,
    norm_gain,
    w_query,
    w_key,
    w_value,
    w_output,
    qkv_in,
    q_out,
    kv_out,
    o_in,
    o_out,
    lengths,
    prompt_adapter,
    adapter_slot,
):
    tok_rows = tokens.shape[0]
    tok_count = lax.axis_size("tok")
    own_count = lax.axis_size("own")
    per_owner = qkv_in.shape[0]
    device_here = lax.axis_index(("tok", "own"))
    positions = device_here * tok_rows + jnp.arange(tok_rows, dtype=jnp.int32)
    segment, offset, members = prompt_index(positions, lengths)
    prompt_count = lengths.shape[0]
    first_segment = segment[0]
    code_rows = segment - first_segment
    normed = rms_norm(tokens, norm_gain)
    tables = (qkv_in, q_out, kv_out, o_in, o_out)
    table_shapes = tuple((table.shape[1:] for table in tables))
    packed = jnp.concatenate([table.reshape(per_owner, -1) for table in tables], axis=1)
    all_slots = lax.all_gather(packed, "own", axis=0, tiled=True)
    own_here = lax.axis_index("own")
    group_blocks = jnp.arange(tok_count, dtype=jnp.int32) * own_count + own_here
    prompt_starts = jnp.cumsum(lengths) - lengths
    group_first = (
        jnp.sum(
            (group_blocks[:, None] * tok_rows >= prompt_starts[None, :]).astype(jnp.int32), axis=1
        )
        - 1
    )
    group_segments = jnp.minimum(
        group_first[:, None] + jnp.arange(SEG_DEV, dtype=jnp.int32)[None, :], prompt_count - 1
    )
    group_slots = jnp.take(adapter_slot, jnp.take(prompt_adapter, group_segments))
    outgoing = jnp.take(all_slots, group_slots.reshape(-1), axis=0).reshape(
        tok_count, SEG_DEV, packed.shape[1]
    )
    split_col = sum(shape[0] * shape[1] for shape in table_shapes[:3])
    incoming = jnp.concatenate(
        [
            lax.all_to_all(outgoing[:, :, :split_col], "tok", 0, 0, tiled=True),
            lax.all_to_all(outgoing[:, :, split_col:], "tok", 0, 0, tiled=True),
        ],
        axis=2,
    )
    selected = []
    col = 0
    for table_shape in table_shapes:
        width = table_shape[0] * table_shape[1]
        piece = incoming[:, :, col : col + width].reshape(
            tok_count, SEG_DEV, table_shape[0], table_shape[1]
        )
        col += width
        selected.append(
            jnp.transpose(piece, (1, 2, 0, 3)).reshape(
                SEG_DEV, table_shape[0], tok_count * table_shape[1]
            )
        )
    input_maps, query_maps, keyvalue_maps, output_in_maps, output_out_maps = selected
    delta_q, delta_k, delta_v = adapter_terms(
        normed,
        code_rows,
        input_maps,
        ((0, query_maps), (RANK, keyvalue_maps[:, :RANK]), (2 * RANK, keyvalue_maps[:, RANK:])),
    )
    base_q = jnp.dot(normed, w_query, preferred_element_type=jnp.float32)
    base_k = jnp.dot(normed, w_key, preferred_element_type=jnp.float32)
    base_v = jnp.dot(normed, w_value, preferred_element_type=jnp.float32)
    query_lin = (base_q + delta_q.astype(jnp.float32)).reshape(tok_rows, HEADS, HEAD_WIDTH)
    queries = rotate(query_lin, offset).reshape(tok_rows, D).astype(jnp.bfloat16)
    key_lin = (base_k + delta_k.astype(jnp.float32)).reshape(tok_rows, KV_HEADS, HEAD_WIDTH)
    key_rows = rotate(key_lin, offset).reshape(tok_rows, KVW).astype(jnp.bfloat16)
    value_rows = (base_v + delta_v.astype(jnp.float32)).astype(jnp.bfloat16)
    key_value = jnp.concatenate([key_rows, value_rows], axis=1)

    held = key_value
    earlier = []
    distance = 1
    while distance < REACH + 1:
        send_blocks = min(distance, REACH + 1 - distance)
        arrived = from_behind(held[held.shape[0] - send_blocks * tok_rows :], ("tok", "own"), distance)
        earlier.insert(0, arrived)
        held = jnp.concatenate([arrived, held], axis=0)
        distance *= 2
    key_positions = (
        device_here * tok_rows
        - REACH * tok_rows
        + jnp.arange((REACH + 1) * tok_rows, dtype=jnp.int32)
    )
    key_segment = prompt_index(key_positions, lengths)[0]
    attn_rows = attend_blocks(queries, earlier + [key_value], segment, key_segment)
    delta_o = adapter_terms(attn_rows, code_rows, output_in_maps, ((0, output_out_maps),))[0]
    projected_out = jnp.dot(
        attn_rows, w_output, preferred_element_type=jnp.float32
    ) + delta_o.astype(jnp.float32)
    mixed_rows = (tokens.astype(jnp.float32) + projected_out).astype(jnp.bfloat16)
    return (mixed_rows, key_value)


def solution(mesh):
    return jax.shard_map(
        on_device,
        mesh=mesh,
        in_specs=(
            P(("tok", "own"), None),
            P(),
            P(),
            P(),
            P(),
            P(),
            P("own", None, "tok"),
            P("own", None, "tok"),
            P("own", None, "tok"),
            P("own", None, "tok"),
            P("own", None, "tok"),
            P(),
            P(),
            P(),
        ),
        out_specs=(P(("tok", "own"), None), P(("tok", "own"), None)),
        check_vma=False,
    )
```

```python
import math

import functools

import jax
import jax.numpy as jnp
from jax import lax
from jax.experimental import pallas as pl
from jax.experimental.pallas import tpu as pltpu
from jax.sharding import PartitionSpec as P

D = 1152
HEADS = 18
KV_HEADS = 6
HEAD_WIDTH = 64
RANK = 16
REACH = 12
KVW = 384
SEG_DEV = 5


EPS = 1e-05
THETA = 10000.0


def from_behind(block, axis, distance):
    devices = range(lax.axis_size(axis))
    route = [(i - distance, i) for i in devices if i - distance in devices]
    return lax.ppermute(block, axis, route)


def rms_norm(row_block, gain_vec):
    widened = row_block.astype(jnp.float32)
    inverse_rms = lax.rsqrt(jnp.mean(widened * widened, axis=-1, keepdims=True) + EPS)
    return (widened * inverse_rms * gain_vec.astype(jnp.float32)).astype(jnp.bfloat16)


def prompt_index(positions, lengths):
    prompt_ends = jnp.cumsum(lengths)
    prompt_starts = prompt_ends - lengths
    inside = (positions[:, None] >= prompt_starts[None, :]).astype(jnp.int32)
    segment = jnp.sum(inside, axis=1) - 1
    members = jnp.arange(lengths.shape[0], dtype=jnp.int32)[None, :] == segment[:, None]
    offset = positions - jnp.sum(jnp.where(members, prompt_starts[None, :], 0), axis=1)
    return (segment, offset, members)


def slot_lookup(adapter, adapter_slot):
    matches = jnp.arange(adapter_slot.shape[0], dtype=jnp.int32)[None, :] == adapter[:, None]
    return jnp.sum(jnp.where(matches, adapter_slot[None, :], 0), axis=1)


def rotate(vectors, offset):
    half_dim = vectors.shape[-1] // 2
    frequency = jnp.exp(
        jnp.arange(half_dim, dtype=jnp.float32) * (-2.0 * math.log(THETA) / vectors.shape[-1])
    )
    angles = offset.astype(jnp.float32)[:, None] * frequency[None, :]
    cosine = jnp.cos(angles)[:, None, :]
    sine_table = jnp.sin(angles)[:, None, :]
    first_half = vectors[..., :half_dim]
    second_half = vectors[..., half_dim:]
    return jnp.concatenate(
        [
            first_half * cosine - second_half * sine_table,
            second_half * cosine + first_half * sine_table,
        ],
        axis=-1,
    )


def adapter_terms(row_block, code_rows, a_in, pieces):
    table_count, rank_cols, in_width = a_in.shape
    projected = lax.dot_general(
        row_block,
        a_in.reshape(table_count * rank_cols, in_width),
        (((1,), (1,)), ((), ())),
        preferred_element_type=jnp.float32,
    )
    chosen = (jnp.arange(table_count, dtype=jnp.int32)[None, :] == code_rows[:, None]).astype(
        jnp.float32
    )
    low_rank = (projected.reshape(-1, table_count, rank_cols) * chosen[:, :, None]).astype(
        jnp.bfloat16
    )
    results = []
    for col_start, b_table in pieces:
        width_rank = b_table.shape[1]
        section = low_rank[:, :, col_start : col_start + width_rank].reshape(
            -1, table_count * width_rank
        )
        results.append(
            jnp.dot(
                section,
                b_table.reshape(table_count * width_rank, b_table.shape[2]),
                preferred_element_type=jnp.float32,
            ).astype(jnp.bfloat16)
        )
    return tuple(results)


def attention_kernel(block_count, query_ref, *refs):
    value_refs = refs[:block_count]
    query_segment_ref, key_segment_ref, out_ref, score_ref = refs[block_count:]
    rows = query_ref.shape[0]
    groups = HEADS // KV_HEADS
    query_segment = query_segment_ref[...]
    row_index = lax.broadcasted_iota(jnp.int32, (rows, rows), 0)
    col_index = lax.broadcasted_iota(jnp.int32, (rows, rows), 1)
    masks = []
    for block in range(block_count):
        same = query_segment == key_segment_ref[:, block * rows : (block + 1) * rows]
        if block == block_count - 1:
            same = same & (col_index <= row_index)
        masks.append(same)
    for kv_head in range(KV_HEADS):
        key_cols = slice(kv_head * HEAD_WIDTH, (kv_head + 1) * HEAD_WIDTH)
        value_cols = slice(KVW + kv_head * HEAD_WIDTH, KVW + (kv_head + 1) * HEAD_WIDTH)
        for group in range(groups):
            head = kv_head * groups + group
            head_cols = slice(head * HEAD_WIDTH, (head + 1) * HEAD_WIDTH)
            query_head = query_ref[:, head_cols]
            for block in range(block_count):
                score = lax.dot_general(
                    query_head,
                    value_refs[block][:, key_cols],
                    (((1,), (1,)), ((), ())),
                    preferred_element_type=jnp.float32,
                ) * HEAD_WIDTH ** (-0.5)
                score_ref[:, block * rows : (block + 1) * rows] = jnp.where(
                    masks[block], score, -1e30
                )
            scores = score_ref[...]
            top_score = jnp.max(scores, axis=1, keepdims=True)
            exp_scores = jnp.exp(scores - top_score)
            row_total = jnp.sum(exp_scores, axis=1, keepdims=True)
            rounded = exp_scores.astype(jnp.bfloat16)
            summed = jnp.zeros((rows, HEAD_WIDTH), jnp.float32)
            for block in range(block_count):
                summed = summed + jnp.dot(
                    rounded[:, block * rows : (block + 1) * rows],
                    value_refs[block][:, value_cols],
                    preferred_element_type=jnp.float32,
                )
            out_ref[:, head_cols] = (summed / row_total).astype(out_ref.dtype)


def attend_blocks(queries, blocks, query_segment, key_segment):
    rows = queries.shape[0]
    block_count = len(blocks)
    keys = block_count * rows
    vmem = pl.BlockSpec(memory_space=pltpu.VMEM)
    return pl.pallas_call(
        functools.partial(attention_kernel, block_count),
        out_shape=jax.ShapeDtypeStruct(queries.shape, jnp.bfloat16),
        in_specs=[vmem] * (block_count + 3),
        out_specs=vmem,
        scratch_shapes=[pltpu.VMEM((rows, keys), jnp.float32)],
        cost_estimate=pl.CostEstimate(
            flops=4 * HEADS * rows * keys * HEAD_WIDTH,
            transcendentals=HEADS * rows * keys,
            bytes_accessed=2 * (2 * queries.size + block_count * blocks[0].size),
        ),
    )(queries, *blocks, query_segment.reshape(rows, 1), key_segment.reshape(1, keys))


def on_device(
    tokens,
    norm_gain,
    w_query,
    w_key,
    w_value,
    w_output,
    qkv_in,
    q_out,
    kv_out,
    o_in,
    o_out,
    lengths,
    prompt_adapter,
    adapter_slot,
):
    tok_rows = tokens.shape[0]
    tok_count = lax.axis_size("tok")
    own_count = lax.axis_size("own")
    per_owner = qkv_in.shape[0]
    device_here = lax.axis_index(("tok", "own"))
    positions = device_here * tok_rows + jnp.arange(tok_rows, dtype=jnp.int32)
    segment, offset, members = prompt_index(positions, lengths)
    prompt_count = lengths.shape[0]
    first_segment = segment[0]
    code_rows = segment - first_segment
    normed = rms_norm(tokens, norm_gain)
    tables = (qkv_in, q_out, kv_out, o_in, o_out)
    table_shapes = tuple((table.shape[1:] for table in tables))
    packed = jnp.concatenate([table.reshape(per_owner, -1) for table in tables], axis=1)
    all_slots = lax.all_gather(packed, "own", axis=0, tiled=True)
    own_here = lax.axis_index("own")
    group_blocks = jnp.arange(tok_count, dtype=jnp.int32) * own_count + own_here
    prompt_starts = jnp.cumsum(lengths) - lengths
    group_first = (
        jnp.sum(
            (group_blocks[:, None] * tok_rows >= prompt_starts[None, :]).astype(jnp.int32), axis=1
        )
        - 1
    )
    group_segments = jnp.minimum(
        group_first[:, None] + jnp.arange(SEG_DEV, dtype=jnp.int32)[None, :], prompt_count - 1
    )
    group_slots = jnp.take(adapter_slot, jnp.take(prompt_adapter, group_segments))
    pick = (
        group_slots.reshape(-1)[:, None]
        == jnp.arange(all_slots.shape[0], dtype=jnp.int32)[None, :]
    ).astype(all_slots.dtype)
    outgoing = (
        jnp.dot(pick, all_slots, preferred_element_type=jnp.float32)
        .astype(all_slots.dtype)
        .reshape(tok_count, SEG_DEV, packed.shape[1])
    )
    split_col = sum(shape[0] * shape[1] for shape in table_shapes[:3])
    incoming = jnp.concatenate(
        [
            lax.all_to_all(outgoing[:, :, :split_col], "tok", 0, 0, tiled=True),
            lax.all_to_all(outgoing[:, :, split_col:], "tok", 0, 0, tiled=True),
        ],
        axis=2,
    )
    selected = []
    col = 0
    for table_shape in table_shapes:
        width = table_shape[0] * table_shape[1]
        piece = incoming[:, :, col : col + width].reshape(
            tok_count, SEG_DEV, table_shape[0], table_shape[1]
        )
        col += width
        selected.append(
            jnp.transpose(piece, (1, 2, 0, 3)).reshape(
                SEG_DEV, table_shape[0], tok_count * table_shape[1]
            )
        )
    input_maps, query_maps, keyvalue_maps, output_in_maps, output_out_maps = selected
    delta_q, delta_k, delta_v = adapter_terms(
        normed,
        code_rows,
        input_maps,
        ((0, query_maps), (RANK, keyvalue_maps[:, :RANK]), (2 * RANK, keyvalue_maps[:, RANK:])),
    )
    base_q = jnp.dot(normed, w_query, preferred_element_type=jnp.float32)
    base_k = jnp.dot(normed, w_key, preferred_element_type=jnp.float32)
    base_v = jnp.dot(normed, w_value, preferred_element_type=jnp.float32)
    query_lin = (base_q + delta_q.astype(jnp.float32)).reshape(tok_rows, HEADS, HEAD_WIDTH)
    queries = rotate(query_lin, offset).reshape(tok_rows, D).astype(jnp.bfloat16)
    key_lin = (base_k + delta_k.astype(jnp.float32)).reshape(tok_rows, KV_HEADS, HEAD_WIDTH)
    key_rows = rotate(key_lin, offset).reshape(tok_rows, KVW).astype(jnp.bfloat16)
    value_rows = (base_v + delta_v.astype(jnp.float32)).astype(jnp.bfloat16)
    key_value = jnp.concatenate([key_rows, value_rows], axis=1)

    earlier = [from_behind(key_value, ("tok", "own"), distance) for distance in range(REACH, 0, -1)]
    key_positions = (
        device_here * tok_rows
        - REACH * tok_rows
        + jnp.arange((REACH + 1) * tok_rows, dtype=jnp.int32)
    )
    key_segment = prompt_index(key_positions, lengths)[0]
    attn_rows = attend_blocks(queries, earlier + [key_value], segment, key_segment)
    delta_o = adapter_terms(attn_rows, code_rows, output_in_maps, ((0, output_out_maps),))[0]
    projected_out = jnp.dot(
        attn_rows, w_output, preferred_element_type=jnp.float32
    ) + delta_o.astype(jnp.float32)
    mixed_rows = (tokens.astype(jnp.float32) + projected_out).astype(jnp.bfloat16)
    return (mixed_rows, key_value)


def solution(mesh):
    return jax.shard_map(
        on_device,
        mesh=mesh,
        in_specs=(
            P(("tok", "own"), None),
            P(),
            P(),
            P(),
            P(),
            P(),
            P("own", None, "tok"),
            P("own", None, "tok"),
            P("own", None, "tok"),
            P("own", None, "tok"),
            P("own", None, "tok"),
            P(),
            P(),
            P(),
        ),
        out_specs=(P(("tok", "own"), None), P(("tok", "own"), None)),
        check_vma=False,
    )
```

```python
import math

import functools

import jax
import jax.numpy as jnp
from jax import lax
from jax.experimental import pallas as pl
from jax.experimental.pallas import tpu as pltpu
from jax.sharding import PartitionSpec as P

D = 1152
HEADS = 18
KV_HEADS = 6
HEAD_WIDTH = 64
RANK = 16
REACH = 12
KVW = 384
SEG_DEV = 5


EPS = 1e-05
THETA = 10000.0


def from_behind(block, axis, distance):
    devices = range(lax.axis_size(axis))
    route = [(i - distance, i) for i in devices if i - distance in devices]
    return lax.ppermute(block, axis, route)


def rms_norm(row_block, gain_vec):
    widened = row_block.astype(jnp.float32)
    inverse_rms = lax.rsqrt(jnp.mean(widened * widened, axis=-1, keepdims=True) + EPS)
    return (widened * inverse_rms * gain_vec.astype(jnp.float32)).astype(jnp.bfloat16)


def prompt_index(positions, lengths):
    prompt_ends = jnp.cumsum(lengths)
    prompt_starts = prompt_ends - lengths
    inside = (positions[:, None] >= prompt_starts[None, :]).astype(jnp.int32)
    segment = jnp.sum(inside, axis=1) - 1
    members = jnp.arange(lengths.shape[0], dtype=jnp.int32)[None, :] == segment[:, None]
    offset = positions - jnp.sum(jnp.where(members, prompt_starts[None, :], 0), axis=1)
    return (segment, offset, members)


def slot_lookup(adapter, adapter_slot):
    matches = jnp.arange(adapter_slot.shape[0], dtype=jnp.int32)[None, :] == adapter[:, None]
    return jnp.sum(jnp.where(matches, adapter_slot[None, :], 0), axis=1)


def rotate(vectors, offset):
    half_dim = vectors.shape[-1] // 2
    frequency = jnp.exp(
        jnp.arange(half_dim, dtype=jnp.float32) * (-2.0 * math.log(THETA) / vectors.shape[-1])
    )
    angles = offset.astype(jnp.float32)[:, None] * frequency[None, :]
    cosine = jnp.cos(angles)[:, None, :]
    sine_table = jnp.sin(angles)[:, None, :]
    first_half = vectors[..., :half_dim]
    second_half = vectors[..., half_dim:]
    return jnp.concatenate(
        [
            first_half * cosine - second_half * sine_table,
            second_half * cosine + first_half * sine_table,
        ],
        axis=-1,
    )


def adapter_terms(row_block, code_rows, a_in, pieces):
    table_count, rank_cols, in_width = a_in.shape
    projected = lax.dot_general(
        row_block,
        a_in.reshape(table_count * rank_cols, in_width),
        (((1,), (1,)), ((), ())),
        preferred_element_type=jnp.float32,
    )
    chosen = (jnp.arange(table_count, dtype=jnp.int32)[None, :] == code_rows[:, None]).astype(
        jnp.float32
    )
    low_rank = (projected.reshape(-1, table_count, rank_cols) * chosen[:, :, None]).astype(
        jnp.bfloat16
    )
    results = []
    for col_start, b_table in pieces:
        width_rank = b_table.shape[1]
        section = low_rank[:, :, col_start : col_start + width_rank].reshape(
            -1, table_count * width_rank
        )
        results.append(
            jnp.dot(
                section,
                b_table.reshape(table_count * width_rank, b_table.shape[2]),
                preferred_element_type=jnp.float32,
            ).astype(jnp.bfloat16)
        )
    return tuple(results)


def attention_kernel(block_count, query_ref, *refs):
    value_refs = refs[:block_count]
    query_segment_ref, key_segment_ref, out_ref = refs[block_count:]
    rows = query_ref.shape[0]
    keys = block_count * rows
    groups = HEADS // KV_HEADS
    query_segment = query_segment_ref[...]
    row_index = lax.broadcasted_iota(jnp.int32, (rows, keys), 0)
    col_index = lax.broadcasted_iota(jnp.int32, (rows, keys), 1)
    allowed = (query_segment == key_segment_ref[...]) & (col_index <= row_index + (keys - rows))
    allowed = jnp.concatenate([allowed] * groups, axis=0)
    for kv_head in range(KV_HEADS):
        key_cols = slice(kv_head * HEAD_WIDTH, (kv_head + 1) * HEAD_WIDTH)
        value_cols = slice(KVW + kv_head * HEAD_WIDTH, KVW + (kv_head + 1) * HEAD_WIDTH)
        key_head = jnp.concatenate([ref[:, key_cols] for ref in value_refs], axis=0)
        value_head = jnp.concatenate([ref[:, value_cols] for ref in value_refs], axis=0)
        query_group = jnp.concatenate(
            [
                query_ref[:, (kv_head * groups + group) * HEAD_WIDTH : (kv_head * groups + group + 1) * HEAD_WIDTH]
                for group in range(groups)
            ],
            axis=0,
        )
        scores = lax.dot_general(
            query_group, key_head, (((1,), (1,)), ((), ())), preferred_element_type=jnp.float32
        ) * HEAD_WIDTH ** (-0.5)
        scores = jnp.where(allowed, scores, -1e30)
        top_score = jnp.max(scores, axis=1, keepdims=True)
        exp_scores = jnp.exp(scores - top_score)
        row_total = jnp.sum(exp_scores, axis=1, keepdims=True)
        summed = jnp.dot(
            exp_scores.astype(jnp.bfloat16), value_head, preferred_element_type=jnp.float32
        )
        attended = (summed / row_total).astype(out_ref.dtype)
        for group in range(groups):
            head = kv_head * groups + group
            out_ref[:, head * HEAD_WIDTH : (head + 1) * HEAD_WIDTH] = attended[
                group * rows : (group + 1) * rows
            ]


def attend_blocks(queries, blocks, query_segment, key_segment):
    rows = queries.shape[0]
    block_count = len(blocks)
    keys = block_count * rows
    vmem = pl.BlockSpec(memory_space=pltpu.VMEM)
    return pl.pallas_call(
        functools.partial(attention_kernel, block_count),
        out_shape=jax.ShapeDtypeStruct(queries.shape, jnp.bfloat16),
        in_specs=[vmem] * (block_count + 3),
        out_specs=vmem,
        cost_estimate=pl.CostEstimate(
            flops=4 * HEADS * rows * keys * HEAD_WIDTH,
            transcendentals=HEADS * rows * keys,
            bytes_accessed=2 * (2 * queries.size + block_count * blocks[0].size),
        ),
    )(queries, *blocks, query_segment.reshape(rows, 1), key_segment.reshape(1, keys))


def on_device(
    tokens,
    norm_gain,
    w_query,
    w_key,
    w_value,
    w_output,
    qkv_in,
    q_out,
    kv_out,
    o_in,
    o_out,
    lengths,
    prompt_adapter,
    adapter_slot,
):
    tok_rows = tokens.shape[0]
    tok_count = lax.axis_size("tok")
    own_count = lax.axis_size("own")
    per_owner = qkv_in.shape[0]
    device_here = lax.axis_index(("tok", "own"))
    positions = device_here * tok_rows + jnp.arange(tok_rows, dtype=jnp.int32)
    segment, offset, members = prompt_index(positions, lengths)
    prompt_count = lengths.shape[0]
    first_segment = segment[0]
    code_rows = segment - first_segment
    normed = rms_norm(tokens, norm_gain)
    tables = (qkv_in, q_out, kv_out, o_in, o_out)
    table_shapes = tuple((table.shape[1:] for table in tables))
    packed = jnp.concatenate([table.reshape(per_owner, -1) for table in tables], axis=1)
    all_slots = lax.all_gather(packed, "own", axis=0, tiled=True)
    own_here = lax.axis_index("own")
    group_blocks = jnp.arange(tok_count, dtype=jnp.int32) * own_count + own_here
    prompt_starts = jnp.cumsum(lengths) - lengths
    group_first = (
        jnp.sum(
            (group_blocks[:, None] * tok_rows >= prompt_starts[None, :]).astype(jnp.int32), axis=1
        )
        - 1
    )
    group_segments = jnp.minimum(
        group_first[:, None] + jnp.arange(SEG_DEV, dtype=jnp.int32)[None, :], prompt_count - 1
    )
    group_slots = jnp.take(adapter_slot, jnp.take(prompt_adapter, group_segments))
    pick = (
        group_slots.reshape(-1)[:, None]
        == jnp.arange(all_slots.shape[0], dtype=jnp.int32)[None, :]
    ).astype(all_slots.dtype)
    outgoing = (
        jnp.dot(pick, all_slots, preferred_element_type=jnp.float32)
        .astype(all_slots.dtype)
        .reshape(tok_count, SEG_DEV, packed.shape[1])
    )
    split_col = sum(shape[0] * shape[1] for shape in table_shapes[:3])
    incoming = jnp.concatenate(
        [
            lax.all_to_all(outgoing[:, :, :split_col], "tok", 0, 0, tiled=True),
            lax.all_to_all(outgoing[:, :, split_col:], "tok", 0, 0, tiled=True),
        ],
        axis=2,
    )
    selected = []
    col = 0
    for table_shape in table_shapes:
        width = table_shape[0] * table_shape[1]
        piece = incoming[:, :, col : col + width].reshape(
            tok_count, SEG_DEV, table_shape[0], table_shape[1]
        )
        col += width
        selected.append(
            jnp.transpose(piece, (1, 2, 0, 3)).reshape(
                SEG_DEV, table_shape[0], tok_count * table_shape[1]
            )
        )
    input_maps, query_maps, keyvalue_maps, output_in_maps, output_out_maps = selected
    delta_q, delta_k, delta_v = adapter_terms(
        normed,
        code_rows,
        input_maps,
        ((0, query_maps), (RANK, keyvalue_maps[:, :RANK]), (2 * RANK, keyvalue_maps[:, RANK:])),
    )
    base_q = jnp.dot(normed, w_query, preferred_element_type=jnp.float32)
    base_k = jnp.dot(normed, w_key, preferred_element_type=jnp.float32)
    base_v = jnp.dot(normed, w_value, preferred_element_type=jnp.float32)
    query_lin = (base_q + delta_q.astype(jnp.float32)).reshape(tok_rows, HEADS, HEAD_WIDTH)
    queries = rotate(query_lin, offset).reshape(tok_rows, D).astype(jnp.bfloat16)
    key_lin = (base_k + delta_k.astype(jnp.float32)).reshape(tok_rows, KV_HEADS, HEAD_WIDTH)
    key_rows = rotate(key_lin, offset).reshape(tok_rows, KVW).astype(jnp.bfloat16)
    value_rows = (base_v + delta_v.astype(jnp.float32)).astype(jnp.bfloat16)
    key_value = jnp.concatenate([key_rows, value_rows], axis=1)

    earlier = [from_behind(key_value, ("tok", "own"), distance) for distance in range(REACH, 0, -1)]
    key_positions = (
        device_here * tok_rows
        - REACH * tok_rows
        + jnp.arange((REACH + 1) * tok_rows, dtype=jnp.int32)
    )
    key_segment = prompt_index(key_positions, lengths)[0]
    attn_rows = attend_blocks(queries, earlier + [key_value], segment, key_segment)
    delta_o = adapter_terms(attn_rows, code_rows, output_in_maps, ((0, output_out_maps),))[0]
    projected_out = jnp.dot(
        attn_rows, w_output, preferred_element_type=jnp.float32
    ) + delta_o.astype(jnp.float32)
    mixed_rows = (tokens.astype(jnp.float32) + projected_out).astype(jnp.bfloat16)
    return (mixed_rows, key_value)


def solution(mesh):
    return jax.shard_map(
        on_device,
        mesh=mesh,
        in_specs=(
            P(("tok", "own"), None),
            P(),
            P(),
            P(),
            P(),
            P(),
            P("own", None, "tok"),
            P("own", None, "tok"),
            P("own", None, "tok"),
            P("own", None, "tok"),
            P("own", None, "tok"),
            P(),
            P(),
            P(),
        ),
        out_specs=(P(("tok", "own"), None), P(("tok", "own"), None)),
        check_vma=False,
    )
```

```python
import math

import functools

import jax
import jax.numpy as jnp
from jax import lax
from jax.experimental import pallas as pl
from jax.experimental.pallas import tpu as pltpu
from jax.sharding import PartitionSpec as P

D = 1152
HEADS = 18
KV_HEADS = 6
HEAD_WIDTH = 64
RANK = 16
REACH = 12
KVW = 384
SEG_DEV = 5


EPS = 1e-05
THETA = 10000.0


def from_behind(block, axis, distance):
    devices = range(lax.axis_size(axis))
    route = [(i - distance, i) for i in devices if i - distance in devices]
    return lax.ppermute(block, axis, route)


def rms_norm(row_block, gain_vec):
    widened = row_block.astype(jnp.float32)
    inverse_rms = lax.rsqrt(jnp.mean(widened * widened, axis=-1, keepdims=True) + EPS)
    return (widened * inverse_rms * gain_vec.astype(jnp.float32)).astype(jnp.bfloat16)


def prompt_index(positions, lengths):
    prompt_ends = jnp.cumsum(lengths)
    prompt_starts = prompt_ends - lengths
    inside = (positions[:, None] >= prompt_starts[None, :]).astype(jnp.int32)
    segment = jnp.sum(inside, axis=1) - 1
    members = jnp.arange(lengths.shape[0], dtype=jnp.int32)[None, :] == segment[:, None]
    offset = positions - jnp.sum(jnp.where(members, prompt_starts[None, :], 0), axis=1)
    return (segment, offset, members)


def slot_lookup(adapter, adapter_slot):
    matches = jnp.arange(adapter_slot.shape[0], dtype=jnp.int32)[None, :] == adapter[:, None]
    return jnp.sum(jnp.where(matches, adapter_slot[None, :], 0), axis=1)


def rotate(vectors, offset):
    half_dim = vectors.shape[-1] // 2
    frequency = jnp.exp(
        jnp.arange(half_dim, dtype=jnp.float32) * (-2.0 * math.log(THETA) / vectors.shape[-1])
    )
    angles = offset.astype(jnp.float32)[:, None] * frequency[None, :]
    cosine = jnp.cos(angles)[:, None, :]
    sine_table = jnp.sin(angles)[:, None, :]
    first_half = vectors[..., :half_dim]
    second_half = vectors[..., half_dim:]
    return jnp.concatenate(
        [
            first_half * cosine - second_half * sine_table,
            second_half * cosine + first_half * sine_table,
        ],
        axis=-1,
    )


def adapter_terms(row_block, code_rows, a_in, pieces):
    table_count, rank_cols, in_width = a_in.shape
    projected = lax.dot_general(
        row_block,
        a_in.reshape(table_count * rank_cols, in_width),
        (((1,), (1,)), ((), ())),
        preferred_element_type=jnp.float32,
    )
    chosen = (jnp.arange(table_count, dtype=jnp.int32)[None, :] == code_rows[:, None]).astype(
        jnp.float32
    )
    low_rank = (projected.reshape(-1, table_count, rank_cols) * chosen[:, :, None]).astype(
        jnp.bfloat16
    )
    results = []
    for col_start, b_table in pieces:
        width_rank = b_table.shape[1]
        section = low_rank[:, :, col_start : col_start + width_rank].reshape(
            -1, table_count * width_rank
        )
        results.append(
            jnp.dot(
                section,
                b_table.reshape(table_count * width_rank, b_table.shape[2]),
                preferred_element_type=jnp.float32,
            ).astype(jnp.bfloat16)
        )
    return tuple(results)


def attention_kernel(block_count, query_ref, *refs):
    value_refs = refs[:block_count]
    query_segment_ref, key_segment_ref, out_ref = refs[block_count:]
    rows = query_ref.shape[0]
    keys = block_count * rows
    groups = HEADS // KV_HEADS
    query_segment = query_segment_ref[...]
    row_index = lax.broadcasted_iota(jnp.int32, (rows, keys), 0)
    col_index = lax.broadcasted_iota(jnp.int32, (rows, keys), 1)
    allowed = (query_segment == key_segment_ref[...]) & (col_index <= row_index + (keys - rows))
    allowed = jnp.concatenate([allowed] * groups, axis=0)
    for kv_head in range(KV_HEADS):
        key_cols = slice(kv_head * HEAD_WIDTH, (kv_head + 1) * HEAD_WIDTH)
        value_cols = slice(KVW + kv_head * HEAD_WIDTH, KVW + (kv_head + 1) * HEAD_WIDTH)
        key_head = jnp.concatenate([ref[:, key_cols] for ref in value_refs], axis=0)
        value_head = jnp.concatenate([ref[:, value_cols] for ref in value_refs], axis=0)
        query_group = jnp.concatenate(
            [
                query_ref[:, (kv_head * groups + group) * HEAD_WIDTH : (kv_head * groups + group + 1) * HEAD_WIDTH]
                for group in range(groups)
            ],
            axis=0,
        )
        scores = lax.dot_general(
            query_group, key_head, (((1,), (1,)), ((), ())), preferred_element_type=jnp.float32
        ) * HEAD_WIDTH ** (-0.5)
        scores = jnp.where(allowed, scores, -1e30)
        top_score = jnp.max(scores, axis=1, keepdims=True)
        exp_scores = jnp.exp(scores - top_score)
        row_total = jnp.sum(exp_scores, axis=1, keepdims=True)
        summed = jnp.dot(
            exp_scores.astype(jnp.bfloat16), value_head, preferred_element_type=jnp.float32
        )
        attended = (summed / row_total).astype(out_ref.dtype)
        for group in range(groups):
            head = kv_head * groups + group
            out_ref[:, head * HEAD_WIDTH : (head + 1) * HEAD_WIDTH] = attended[
                group * rows : (group + 1) * rows
            ]


def attend_blocks(queries, blocks, query_segment, key_segment):
    rows = queries.shape[0]
    block_count = len(blocks)
    keys = block_count * rows
    vmem = pl.BlockSpec(memory_space=pltpu.VMEM)
    return pl.pallas_call(
        functools.partial(attention_kernel, block_count),
        out_shape=jax.ShapeDtypeStruct(queries.shape, jnp.bfloat16),
        in_specs=[vmem] * (block_count + 3),
        out_specs=vmem,
        cost_estimate=pl.CostEstimate(
            flops=4 * HEADS * rows * keys * HEAD_WIDTH,
            transcendentals=HEADS * rows * keys,
            bytes_accessed=2 * (2 * queries.size + block_count * blocks[0].size),
        ),
    )(queries, *blocks, query_segment.reshape(rows, 1), key_segment.reshape(1, keys))


def on_device(
    tokens,
    norm_gain,
    w_query,
    w_key,
    w_value,
    w_output,
    qkv_in,
    q_out,
    kv_out,
    o_in,
    o_out,
    lengths,
    prompt_adapter,
    adapter_slot,
):
    tok_rows = tokens.shape[0]
    tok_count = lax.axis_size("tok")
    own_count = lax.axis_size("own")
    per_owner = qkv_in.shape[0]
    device_here = lax.axis_index(("tok", "own"))
    positions = device_here * tok_rows + jnp.arange(tok_rows, dtype=jnp.int32)
    segment, offset, members = prompt_index(positions, lengths)
    prompt_count = lengths.shape[0]
    first_segment = segment[0]
    code_rows = segment - first_segment
    normed = rms_norm(tokens, norm_gain)
    tables = (
        qkv_in[:, RANK:],
        kv_out,
        qkv_in[:, :RANK],
        q_out,
        o_in,
        o_out,
    )
    table_shapes = tuple((table.shape[1:] for table in tables))
    packed = jnp.concatenate([table.reshape(per_owner, -1) for table in tables], axis=1)
    all_slots = lax.all_gather(packed, "own", axis=0, tiled=True)
    own_here = lax.axis_index("own")
    group_blocks = jnp.arange(tok_count, dtype=jnp.int32) * own_count + own_here
    prompt_starts = jnp.cumsum(lengths) - lengths
    group_first = (
        jnp.sum(
            (group_blocks[:, None] * tok_rows >= prompt_starts[None, :]).astype(jnp.int32), axis=1
        )
        - 1
    )
    group_segments = jnp.minimum(
        group_first[:, None] + jnp.arange(SEG_DEV, dtype=jnp.int32)[None, :], prompt_count - 1
    )
    group_slots = jnp.take(adapter_slot, jnp.take(prompt_adapter, group_segments))
    pick = (
        group_slots.reshape(-1)[:, None]
        == jnp.arange(all_slots.shape[0], dtype=jnp.int32)[None, :]
    ).astype(all_slots.dtype)
    outgoing = (
        jnp.dot(pick, all_slots, preferred_element_type=jnp.float32)
        .astype(all_slots.dtype)
        .reshape(tok_count, SEG_DEV, packed.shape[1])
    )
    split_col = sum(shape[0] * shape[1] for shape in table_shapes[:2])

    def unpack(incoming, shapes):
        pieces = []
        col = 0
        for table_shape in shapes:
            width = table_shape[0] * table_shape[1]
            piece = incoming[:, :, col : col + width].reshape(
                tok_count, SEG_DEV, table_shape[0], table_shape[1]
            )
            col += width
            pieces.append(
                jnp.transpose(piece, (1, 2, 0, 3)).reshape(
                    SEG_DEV, table_shape[0], tok_count * table_shape[1]
                )
            )
        return pieces

    kv_in_maps, keyvalue_maps = unpack(
        lax.all_to_all(outgoing[:, :, :split_col], "tok", 0, 0, tiled=True), table_shapes[:2]
    )
    delta_k, delta_v = adapter_terms(
        normed,
        code_rows,
        kv_in_maps,
        ((0, keyvalue_maps[:, :RANK]), (RANK, keyvalue_maps[:, RANK:])),
    )
    base_k = jnp.dot(normed, w_key, preferred_element_type=jnp.float32)
    base_v = jnp.dot(normed, w_value, preferred_element_type=jnp.float32)
    key_lin = (base_k + delta_k.astype(jnp.float32)).reshape(tok_rows, KV_HEADS, HEAD_WIDTH)
    key_rows = rotate(key_lin, offset).reshape(tok_rows, KVW).astype(jnp.bfloat16)
    value_rows = (base_v + delta_v.astype(jnp.float32)).astype(jnp.bfloat16)
    key_value = jnp.concatenate([key_rows, value_rows], axis=1)
    key_value, outgoing_rest = lax.optimization_barrier((key_value, outgoing[:, :, split_col:]))
    query_in_maps, query_maps, output_in_maps, output_out_maps = unpack(
        lax.all_to_all(outgoing_rest, "tok", 0, 0, tiled=True), table_shapes[2:]
    )
    (delta_q,) = adapter_terms(normed, code_rows, query_in_maps, ((0, query_maps),))
    base_q = jnp.dot(normed, w_query, preferred_element_type=jnp.float32)
    query_lin = (base_q + delta_q.astype(jnp.float32)).reshape(tok_rows, HEADS, HEAD_WIDTH)
    queries = rotate(query_lin, offset).reshape(tok_rows, D).astype(jnp.bfloat16)

    earlier = [from_behind(key_value, ("tok", "own"), distance) for distance in range(REACH, 0, -1)]
    key_positions = (
        device_here * tok_rows
        - REACH * tok_rows
        + jnp.arange((REACH + 1) * tok_rows, dtype=jnp.int32)
    )
    key_segment = prompt_index(key_positions, lengths)[0]
    attn_rows = attend_blocks(queries, earlier + [key_value], segment, key_segment)
    delta_o = adapter_terms(attn_rows, code_rows, output_in_maps, ((0, output_out_maps),))[0]
    projected_out = jnp.dot(
        attn_rows, w_output, preferred_element_type=jnp.float32
    ) + delta_o.astype(jnp.float32)
    mixed_rows = (tokens.astype(jnp.float32) + projected_out).astype(jnp.bfloat16)
    return (mixed_rows, key_value)


def solution(mesh):
    return jax.shard_map(
        on_device,
        mesh=mesh,
        in_specs=(
            P(("tok", "own"), None),
            P(),
            P(),
            P(),
            P(),
            P(),
            P("own", None, "tok"),
            P("own", None, "tok"),
            P("own", None, "tok"),
            P("own", None, "tok"),
            P("own", None, "tok"),
            P(),
            P(),
            P(),
        ),
        out_specs=(P(("tok", "own"), None), P(("tok", "own"), None)),
        check_vma=False,
    )
```

```python
import math

import functools

import jax
import jax.numpy as jnp
from jax import lax
from jax.experimental import pallas as pl
from jax.experimental.pallas import tpu as pltpu
from jax.sharding import PartitionSpec as P

D = 1152
HEADS = 18
KV_HEADS = 6
HEAD_WIDTH = 64
RANK = 16
REACH = 12
KVW = 384
SEG_DEV = 5


EPS = 1e-05
THETA = 10000.0


def from_behind(block, axis, distance):
    devices = range(lax.axis_size(axis))
    route = [(i - distance, i) for i in devices if i - distance in devices]
    return lax.ppermute(block, axis, route)


def rms_norm(row_block, gain_vec):
    widened = row_block.astype(jnp.float32)
    inverse_rms = lax.rsqrt(jnp.mean(widened * widened, axis=-1, keepdims=True) + EPS)
    return (widened * inverse_rms * gain_vec.astype(jnp.float32)).astype(jnp.bfloat16)


def prompt_index(positions, lengths):
    prompt_ends = jnp.cumsum(lengths)
    prompt_starts = prompt_ends - lengths
    inside = (positions[:, None] >= prompt_starts[None, :]).astype(jnp.int32)
    segment = jnp.sum(inside, axis=1) - 1
    members = jnp.arange(lengths.shape[0], dtype=jnp.int32)[None, :] == segment[:, None]
    offset = positions - jnp.sum(jnp.where(members, prompt_starts[None, :], 0), axis=1)
    return (segment, offset, members)


def slot_lookup(adapter, adapter_slot):
    matches = jnp.arange(adapter_slot.shape[0], dtype=jnp.int32)[None, :] == adapter[:, None]
    return jnp.sum(jnp.where(matches, adapter_slot[None, :], 0), axis=1)


def rotate(vectors, offset):
    half_dim = vectors.shape[-1] // 2
    frequency = jnp.exp(
        jnp.arange(half_dim, dtype=jnp.float32) * (-2.0 * math.log(THETA) / vectors.shape[-1])
    )
    angles = offset.astype(jnp.float32)[:, None] * frequency[None, :]
    cosine = jnp.cos(angles)[:, None, :]
    sine_table = jnp.sin(angles)[:, None, :]
    first_half = vectors[..., :half_dim]
    second_half = vectors[..., half_dim:]
    return jnp.concatenate(
        [
            first_half * cosine - second_half * sine_table,
            second_half * cosine + first_half * sine_table,
        ],
        axis=-1,
    )


def adapter_terms(row_block, code_rows, a_in, pieces):
    table_count, rank_cols, in_width = a_in.shape
    projected = lax.dot_general(
        row_block,
        a_in.reshape(table_count * rank_cols, in_width),
        (((1,), (1,)), ((), ())),
        preferred_element_type=jnp.float32,
    )
    chosen = (jnp.arange(table_count, dtype=jnp.int32)[None, :] == code_rows[:, None]).astype(
        jnp.float32
    )
    low_rank = (projected.reshape(-1, table_count, rank_cols) * chosen[:, :, None]).astype(
        jnp.bfloat16
    )
    results = []
    for col_start, b_table in pieces:
        width_rank = b_table.shape[1]
        section = low_rank[:, :, col_start : col_start + width_rank].reshape(
            -1, table_count * width_rank
        )
        results.append(
            jnp.dot(
                section,
                b_table.reshape(table_count * width_rank, b_table.shape[2]),
                preferred_element_type=jnp.float32,
            ).astype(jnp.bfloat16)
        )
    return tuple(results)


def attention_kernel(block_count, query_ref, *refs):
    value_refs = refs[:block_count]
    query_segment_ref, key_segment_ref, out_ref = refs[block_count:]
    rows = query_ref.shape[0]
    keys = block_count * rows
    groups = HEADS // KV_HEADS
    query_segment = query_segment_ref[...]
    row_index = lax.broadcasted_iota(jnp.int32, (rows, keys), 0)
    col_index = lax.broadcasted_iota(jnp.int32, (rows, keys), 1)
    allowed = (query_segment == key_segment_ref[...]) & (col_index <= row_index + (keys - rows))
    allowed = jnp.concatenate([allowed] * groups, axis=0)
    for kv_head in range(KV_HEADS):
        key_cols = slice(kv_head * HEAD_WIDTH, (kv_head + 1) * HEAD_WIDTH)
        value_cols = slice(KVW + kv_head * HEAD_WIDTH, KVW + (kv_head + 1) * HEAD_WIDTH)
        key_head = jnp.concatenate([ref[:, key_cols] for ref in value_refs], axis=0)
        value_head = jnp.concatenate([ref[:, value_cols] for ref in value_refs], axis=0)
        query_group = jnp.concatenate(
            [
                query_ref[:, (kv_head * groups + group) * HEAD_WIDTH : (kv_head * groups + group + 1) * HEAD_WIDTH]
                for group in range(groups)
            ],
            axis=0,
        )
        scores = lax.dot_general(
            query_group, key_head, (((1,), (1,)), ((), ())), preferred_element_type=jnp.float32
        ) * HEAD_WIDTH ** (-0.5)
        scores = jnp.where(allowed, scores, -1e30)
        top_score = jnp.max(scores, axis=1, keepdims=True)
        exp_scores = jnp.exp(scores - top_score)
        row_total = jnp.sum(exp_scores, axis=1, keepdims=True)
        summed = jnp.dot(
            exp_scores.astype(jnp.bfloat16), value_head, preferred_element_type=jnp.float32
        )
        attended = (summed / row_total).astype(out_ref.dtype)
        for group in range(groups):
            head = kv_head * groups + group
            out_ref[:, head * HEAD_WIDTH : (head + 1) * HEAD_WIDTH] = attended[
                group * rows : (group + 1) * rows
            ]


def attend_blocks(queries, blocks, query_segment, key_segment):
    rows = queries.shape[0]
    block_count = len(blocks)
    keys = block_count * rows
    vmem = pl.BlockSpec(memory_space=pltpu.VMEM)
    return pl.pallas_call(
        functools.partial(attention_kernel, block_count),
        out_shape=jax.ShapeDtypeStruct(queries.shape, jnp.bfloat16),
        in_specs=[vmem] * (block_count + 3),
        out_specs=vmem,
        cost_estimate=pl.CostEstimate(
            flops=4 * HEADS * rows * keys * HEAD_WIDTH,
            transcendentals=HEADS * rows * keys,
            bytes_accessed=2 * (2 * queries.size + block_count * blocks[0].size),
        ),
    )(queries, *blocks, query_segment.reshape(rows, 1), key_segment.reshape(1, keys))


def on_device(
    tokens,
    norm_gain,
    w_query,
    w_key,
    w_value,
    w_output,
    qkv_in,
    q_out,
    kv_out,
    o_in,
    o_out,
    lengths,
    prompt_adapter,
    adapter_slot,
):
    tok_rows = tokens.shape[0]
    tok_count = lax.axis_size("tok")
    own_count = lax.axis_size("own")
    per_owner = qkv_in.shape[0]
    device_here = lax.axis_index(("tok", "own"))
    positions = device_here * tok_rows + jnp.arange(tok_rows, dtype=jnp.int32)
    segment, offset, members = prompt_index(positions, lengths)
    prompt_count = lengths.shape[0]
    first_segment = segment[0]
    code_rows = segment - first_segment
    normed = rms_norm(tokens, norm_gain)
    tables = (qkv_in, q_out, kv_out, o_in, o_out)
    table_shapes = tuple((table.shape[1:] for table in tables))
    packed = jnp.concatenate([table.reshape(per_owner, -1) for table in tables], axis=1)
    all_slots = lax.all_gather(packed, "own", axis=0, tiled=True)
    own_here = lax.axis_index("own")
    group_blocks = jnp.arange(tok_count, dtype=jnp.int32) * own_count + own_here
    prompt_starts = jnp.cumsum(lengths) - lengths
    group_first = (
        jnp.sum(
            (group_blocks[:, None] * tok_rows >= prompt_starts[None, :]).astype(jnp.int32), axis=1
        )
        - 1
    )
    group_segments = jnp.minimum(
        group_first[:, None] + jnp.arange(SEG_DEV, dtype=jnp.int32)[None, :], prompt_count - 1
    )
    group_adapter = jnp.sum(
        jnp.where(
            group_segments[:, :, None] == jnp.arange(prompt_count, dtype=jnp.int32)[None, None, :],
            prompt_adapter[None, None, :],
            0,
        ),
        axis=2,
    )
    group_slots = jnp.sum(
        jnp.where(
            group_adapter[:, :, None]
            == jnp.arange(adapter_slot.shape[0], dtype=jnp.int32)[None, None, :],
            adapter_slot[None, None, :],
            0,
        ),
        axis=2,
    )
    split_col = sum(shape[0] * shape[1] for shape in table_shapes[:3])

    def send_rows(cols):
        rows_out = []
        for seg in range(SEG_DEV):
            pick = (
                group_slots[:, seg][:, None]
                == jnp.arange(all_slots.shape[0], dtype=jnp.int32)[None, :]
            ).astype(all_slots.dtype)
            rows_out.append(
                jnp.dot(pick, all_slots[:, cols], preferred_element_type=jnp.float32).astype(
                    all_slots.dtype
                )
            )
        return jnp.concatenate(rows_out, axis=1)

    parts = (
        (slice(0, split_col), table_shapes[:3]),
        (slice(split_col, packed.shape[1]), table_shapes[3:]),
    )
    selected = []
    for cols, shapes in parts:
        width_all = cols.stop - cols.start
        incoming = lax.all_to_all(send_rows(cols), "tok", 0, 0, tiled=True).reshape(
            tok_count, SEG_DEV, width_all
        )
        col = 0
        for table_shape in shapes:
            width = table_shape[0] * table_shape[1]
            piece = incoming[:, :, col : col + width].reshape(
                tok_count, SEG_DEV, table_shape[0], table_shape[1]
            )
            col += width
            selected.append(
                jnp.transpose(piece, (1, 2, 0, 3)).reshape(
                    SEG_DEV, table_shape[0], tok_count * table_shape[1]
                )
            )
    input_maps, query_maps, keyvalue_maps, output_in_maps, output_out_maps = selected
    delta_q, delta_k, delta_v = adapter_terms(
        normed,
        code_rows,
        input_maps,
        ((0, query_maps), (RANK, keyvalue_maps[:, :RANK]), (2 * RANK, keyvalue_maps[:, RANK:])),
    )
    base_q = jnp.dot(normed, w_query, preferred_element_type=jnp.float32)
    base_k = jnp.dot(normed, w_key, preferred_element_type=jnp.float32)
    base_v = jnp.dot(normed, w_value, preferred_element_type=jnp.float32)
    query_lin = (base_q + delta_q.astype(jnp.float32)).reshape(tok_rows, HEADS, HEAD_WIDTH)
    queries = rotate(query_lin, offset).reshape(tok_rows, D).astype(jnp.bfloat16)
    key_lin = (base_k + delta_k.astype(jnp.float32)).reshape(tok_rows, KV_HEADS, HEAD_WIDTH)
    key_rows = rotate(key_lin, offset).reshape(tok_rows, KVW).astype(jnp.bfloat16)
    value_rows = (base_v + delta_v.astype(jnp.float32)).astype(jnp.bfloat16)
    key_value = jnp.concatenate([key_rows, value_rows], axis=1)

    earlier = [from_behind(key_value, ("tok", "own"), distance) for distance in range(REACH, 0, -1)]
    key_positions = (
        device_here * tok_rows
        - REACH * tok_rows
        + jnp.arange((REACH + 1) * tok_rows, dtype=jnp.int32)
    )
    key_segment = prompt_index(key_positions, lengths)[0]
    attn_rows = attend_blocks(queries, earlier + [key_value], segment, key_segment)
    delta_o = adapter_terms(attn_rows, code_rows, output_in_maps, ((0, output_out_maps),))[0]
    projected_out = jnp.dot(
        attn_rows, w_output, preferred_element_type=jnp.float32
    ) + delta_o.astype(jnp.float32)
    mixed_rows = (tokens.astype(jnp.float32) + projected_out).astype(jnp.bfloat16)
    return (mixed_rows, key_value)


def solution(mesh):
    return jax.shard_map(
        on_device,
        mesh=mesh,
        in_specs=(
            P(("tok", "own"), None),
            P(),
            P(),
            P(),
            P(),
            P(),
            P("own", None, "tok"),
            P("own", None, "tok"),
            P("own", None, "tok"),
            P("own", None, "tok"),
            P("own", None, "tok"),
            P(),
            P(),
            P(),
        ),
        out_specs=(P(("tok", "own"), None), P(("tok", "own"), None)),
        check_vma=False,
    )
```

```python
import math

import functools

import jax
import jax.numpy as jnp
from jax import lax
from jax.experimental import pallas as pl
from jax.experimental.pallas import tpu as pltpu
from jax.sharding import PartitionSpec as P

D = 1152
HEADS = 18
KV_HEADS = 6
HEAD_WIDTH = 64
RANK = 16
REACH = 12
KVW = 384
SEG_DEV = 5


EPS = 1e-05
THETA = 10000.0


def from_behind(block, axis, distance):
    devices = range(lax.axis_size(axis))
    route = [(i - distance, i) for i in devices if i - distance in devices]
    return lax.ppermute(block, axis, route)


def rms_norm(row_block, gain_vec):
    widened = row_block.astype(jnp.float32)
    inverse_rms = lax.rsqrt(jnp.mean(widened * widened, axis=-1, keepdims=True) + EPS)
    return (widened * inverse_rms * gain_vec.astype(jnp.float32)).astype(jnp.bfloat16)


def prompt_index(positions, lengths):
    prompt_ends = jnp.cumsum(lengths)
    prompt_starts = prompt_ends - lengths
    inside = (positions[:, None] >= prompt_starts[None, :]).astype(jnp.int32)
    segment = jnp.sum(inside, axis=1) - 1
    members = jnp.arange(lengths.shape[0], dtype=jnp.int32)[None, :] == segment[:, None]
    offset = positions - jnp.sum(jnp.where(members, prompt_starts[None, :], 0), axis=1)
    return (segment, offset, members)


def slot_lookup(adapter, adapter_slot):
    matches = jnp.arange(adapter_slot.shape[0], dtype=jnp.int32)[None, :] == adapter[:, None]
    return jnp.sum(jnp.where(matches, adapter_slot[None, :], 0), axis=1)


def rotate(vectors, offset):
    half_dim = vectors.shape[-1] // 2
    frequency = jnp.exp(
        jnp.arange(half_dim, dtype=jnp.float32) * (-2.0 * math.log(THETA) / vectors.shape[-1])
    )
    angles = offset.astype(jnp.float32)[:, None] * frequency[None, :]
    cosine = jnp.cos(angles)[:, None, :]
    sine_table = jnp.sin(angles)[:, None, :]
    first_half = vectors[..., :half_dim]
    second_half = vectors[..., half_dim:]
    return jnp.concatenate(
        [
            first_half * cosine - second_half * sine_table,
            second_half * cosine + first_half * sine_table,
        ],
        axis=-1,
    )


def adapter_terms(row_block, code_rows, a_in, pieces):
    table_count, rank_cols, in_width = a_in.shape
    projected = lax.dot_general(
        row_block,
        a_in.reshape(table_count * rank_cols, in_width),
        (((1,), (1,)), ((), ())),
        preferred_element_type=jnp.float32,
    )
    chosen = (jnp.arange(table_count, dtype=jnp.int32)[None, :] == code_rows[:, None]).astype(
        jnp.float32
    )
    low_rank = (projected.reshape(-1, table_count, rank_cols) * chosen[:, :, None]).astype(
        jnp.bfloat16
    )
    results = []
    for col_start, b_table in pieces:
        width_rank = b_table.shape[1]
        section = low_rank[:, :, col_start : col_start + width_rank].reshape(
            -1, table_count * width_rank
        )
        results.append(
            jnp.dot(
                section,
                b_table.reshape(table_count * width_rank, b_table.shape[2]),
                preferred_element_type=jnp.float32,
            ).astype(jnp.bfloat16)
        )
    return tuple(results)


def adapter_terms_pieces(row_block, code_rows, a_pieces, pieces):
    piece_count, table_count, rank_cols, in_width = a_pieces.shape
    projected = jnp.einsum(
        "ntc,tsrc->nsr",
        row_block.reshape(row_block.shape[0], piece_count, in_width),
        a_pieces,
        preferred_element_type=jnp.float32,
    )
    chosen = (jnp.arange(table_count, dtype=jnp.int32)[None, :] == code_rows[:, None]).astype(
        jnp.float32
    )
    low_rank = (projected * chosen[:, :, None]).astype(jnp.bfloat16)
    results = []
    for col_start, b_pieces in pieces:
        width_rank = b_pieces.shape[2]
        section = low_rank[:, :, col_start : col_start + width_rank]
        results.append(
            jnp.einsum("nsr,tsrc->ntc", section, b_pieces, preferred_element_type=jnp.float32)
            .reshape(row_block.shape[0], -1)
            .astype(jnp.bfloat16)
        )
    return tuple(results)


def attention_kernel(block_count, query_ref, *refs):
    value_refs = refs[:block_count]
    query_segment_ref, key_segment_ref, out_ref = refs[block_count:]
    rows = query_ref.shape[0]
    keys = block_count * rows
    groups = HEADS // KV_HEADS
    query_segment = query_segment_ref[...]
    row_index = lax.broadcasted_iota(jnp.int32, (rows, keys), 0)
    col_index = lax.broadcasted_iota(jnp.int32, (rows, keys), 1)
    allowed = (query_segment == key_segment_ref[...]) & (col_index <= row_index + (keys - rows))
    allowed = jnp.concatenate([allowed] * groups, axis=0)
    for kv_head in range(KV_HEADS):
        key_cols = slice(kv_head * HEAD_WIDTH, (kv_head + 1) * HEAD_WIDTH)
        value_cols = slice(KVW + kv_head * HEAD_WIDTH, KVW + (kv_head + 1) * HEAD_WIDTH)
        key_head = jnp.concatenate([ref[:, key_cols] for ref in value_refs], axis=0)
        value_head = jnp.concatenate([ref[:, value_cols] for ref in value_refs], axis=0)
        query_group = jnp.concatenate(
            [
                query_ref[:, (kv_head * groups + group) * HEAD_WIDTH : (kv_head * groups + group + 1) * HEAD_WIDTH]
                for group in range(groups)
            ],
            axis=0,
        )
        scores = lax.dot_general(
            query_group, key_head, (((1,), (1,)), ((), ())), preferred_element_type=jnp.float32
        ) * HEAD_WIDTH ** (-0.5)
        scores = jnp.where(allowed, scores, -1e30)
        top_score = jnp.max(scores, axis=1, keepdims=True)
        exp_scores = jnp.exp(scores - top_score)
        row_total = jnp.sum(exp_scores, axis=1, keepdims=True)
        summed = jnp.dot(
            exp_scores.astype(jnp.bfloat16), value_head, preferred_element_type=jnp.float32
        )
        attended = (summed / row_total).astype(out_ref.dtype)
        for group in range(groups):
            head = kv_head * groups + group
            out_ref[:, head * HEAD_WIDTH : (head + 1) * HEAD_WIDTH] = attended[
                group * rows : (group + 1) * rows
            ]


def attend_blocks(queries, blocks, query_segment, key_segment):
    rows = queries.shape[0]
    block_count = len(blocks)
    keys = block_count * rows
    vmem = pl.BlockSpec(memory_space=pltpu.VMEM)
    return pl.pallas_call(
        functools.partial(attention_kernel, block_count),
        out_shape=jax.ShapeDtypeStruct(queries.shape, jnp.bfloat16),
        in_specs=[vmem] * (block_count + 3),
        out_specs=vmem,
        cost_estimate=pl.CostEstimate(
            flops=4 * HEADS * rows * keys * HEAD_WIDTH,
            transcendentals=HEADS * rows * keys,
            bytes_accessed=2 * (2 * queries.size + block_count * blocks[0].size),
        ),
    )(queries, *blocks, query_segment.reshape(rows, 1), key_segment.reshape(1, keys))


def on_device(
    tokens,
    norm_gain,
    w_query,
    w_key,
    w_value,
    w_output,
    qkv_in,
    q_out,
    kv_out,
    o_in,
    o_out,
    lengths,
    prompt_adapter,
    adapter_slot,
):
    tok_rows = tokens.shape[0]
    tok_count = lax.axis_size("tok")
    own_count = lax.axis_size("own")
    per_owner = qkv_in.shape[0]
    device_here = lax.axis_index(("tok", "own"))
    positions = device_here * tok_rows + jnp.arange(tok_rows, dtype=jnp.int32)
    segment, offset, members = prompt_index(positions, lengths)
    prompt_count = lengths.shape[0]
    first_segment = segment[0]
    code_rows = segment - first_segment
    normed = rms_norm(tokens, norm_gain)
    tables = (qkv_in, q_out, kv_out, o_in, o_out)
    table_shapes = tuple((table.shape[1:] for table in tables))
    packed = jnp.concatenate([table.reshape(per_owner, -1) for table in tables], axis=1)
    all_slots = lax.all_gather(packed, "own", axis=0, tiled=True)
    own_here = lax.axis_index("own")
    group_blocks = jnp.arange(tok_count, dtype=jnp.int32) * own_count + own_here
    prompt_starts = jnp.cumsum(lengths) - lengths
    group_first = (
        jnp.sum(
            (group_blocks[:, None] * tok_rows >= prompt_starts[None, :]).astype(jnp.int32), axis=1
        )
        - 1
    )
    group_segments = jnp.minimum(
        group_first[:, None] + jnp.arange(SEG_DEV, dtype=jnp.int32)[None, :], prompt_count - 1
    )
    group_slots = jnp.take(adapter_slot, jnp.take(prompt_adapter, group_segments))
    pick = (
        group_slots.reshape(-1)[:, None]
        == jnp.arange(all_slots.shape[0], dtype=jnp.int32)[None, :]
    ).astype(all_slots.dtype)
    outgoing = (
        jnp.dot(pick, all_slots, preferred_element_type=jnp.float32)
        .astype(all_slots.dtype)
        .reshape(tok_count, SEG_DEV, packed.shape[1])
    )
    split_col = sum(shape[0] * shape[1] for shape in table_shapes[:3])
    incoming = jnp.concatenate(
        [
            lax.all_to_all(outgoing[:, :, :split_col], "tok", 0, 0, tiled=True),
            lax.all_to_all(outgoing[:, :, split_col:], "tok", 0, 0, tiled=True),
        ],
        axis=2,
    )
    selected = []
    col = 0
    for table_shape in table_shapes:
        width = table_shape[0] * table_shape[1]
        piece = incoming[:, :, col : col + width].reshape(
            tok_count, SEG_DEV, table_shape[0], table_shape[1]
        )
        col += width
        selected.append(piece)
    input_maps, query_maps, keyvalue_maps, output_in_maps, output_out_maps = selected
    delta_q, delta_k, delta_v = adapter_terms_pieces(
        normed,
        code_rows,
        input_maps,
        (
            (0, query_maps),
            (RANK, keyvalue_maps[:, :, :RANK]),
            (2 * RANK, keyvalue_maps[:, :, RANK:]),
        ),
    )
    base_q = jnp.dot(normed, w_query, preferred_element_type=jnp.float32)
    base_k = jnp.dot(normed, w_key, preferred_element_type=jnp.float32)
    base_v = jnp.dot(normed, w_value, preferred_element_type=jnp.float32)
    query_lin = (base_q + delta_q.astype(jnp.float32)).reshape(tok_rows, HEADS, HEAD_WIDTH)
    queries = rotate(query_lin, offset).reshape(tok_rows, D).astype(jnp.bfloat16)
    key_lin = (base_k + delta_k.astype(jnp.float32)).reshape(tok_rows, KV_HEADS, HEAD_WIDTH)
    key_rows = rotate(key_lin, offset).reshape(tok_rows, KVW).astype(jnp.bfloat16)
    value_rows = (base_v + delta_v.astype(jnp.float32)).astype(jnp.bfloat16)
    key_value = jnp.concatenate([key_rows, value_rows], axis=1)

    earlier = [from_behind(key_value, ("tok", "own"), distance) for distance in range(REACH, 0, -1)]
    key_positions = (
        device_here * tok_rows
        - REACH * tok_rows
        + jnp.arange((REACH + 1) * tok_rows, dtype=jnp.int32)
    )
    key_segment = prompt_index(key_positions, lengths)[0]
    attn_rows = attend_blocks(queries, earlier + [key_value], segment, key_segment)
    delta_o = adapter_terms_pieces(attn_rows, code_rows, output_in_maps, ((0, output_out_maps),))[0]
    projected_out = jnp.dot(
        attn_rows, w_output, preferred_element_type=jnp.float32
    ) + delta_o.astype(jnp.float32)
    mixed_rows = (tokens.astype(jnp.float32) + projected_out).astype(jnp.bfloat16)
    return (mixed_rows, key_value)


def solution(mesh):
    return jax.shard_map(
        on_device,
        mesh=mesh,
        in_specs=(
            P(("tok", "own"), None),
            P(),
            P(),
            P(),
            P(),
            P(),
            P("own", None, "tok"),
            P("own", None, "tok"),
            P("own", None, "tok"),
            P("own", None, "tok"),
            P("own", None, "tok"),
            P(),
            P(),
            P(),
        ),
        out_specs=(P(("tok", "own"), None), P(("tok", "own"), None)),
        check_vma=False,
    )
```

```python
import math

import functools

import jax
import jax.numpy as jnp
from jax import lax
from jax.experimental import pallas as pl
from jax.experimental.pallas import tpu as pltpu
from jax.sharding import PartitionSpec as P

D = 1152
HEADS = 18
KV_HEADS = 6
HEAD_WIDTH = 64
RANK = 16
REACH = 12
KVW = 384
SEG_DEV = 5


EPS = 1e-05
THETA = 10000.0


def from_behind(block, axis, distance):
    devices = range(lax.axis_size(axis))
    route = [(i - distance, i) for i in devices if i - distance in devices]
    return lax.ppermute(block, axis, route)


def rms_norm(row_block, gain_vec):
    widened = row_block.astype(jnp.float32)
    inverse_rms = lax.rsqrt(jnp.mean(widened * widened, axis=-1, keepdims=True) + EPS)
    return (widened * inverse_rms * gain_vec.astype(jnp.float32)).astype(jnp.bfloat16)


def prompt_index(positions, lengths):
    prompt_ends = jnp.cumsum(lengths)
    prompt_starts = prompt_ends - lengths
    inside = (positions[:, None] >= prompt_starts[None, :]).astype(jnp.int32)
    segment = jnp.sum(inside, axis=1) - 1
    members = jnp.arange(lengths.shape[0], dtype=jnp.int32)[None, :] == segment[:, None]
    offset = positions - jnp.sum(jnp.where(members, prompt_starts[None, :], 0), axis=1)
    return (segment, offset, members)


def slot_lookup(adapter, adapter_slot):
    matches = jnp.arange(adapter_slot.shape[0], dtype=jnp.int32)[None, :] == adapter[:, None]
    return jnp.sum(jnp.where(matches, adapter_slot[None, :], 0), axis=1)


def rotate(vectors, offset):
    half_dim = vectors.shape[-1] // 2
    frequency = jnp.exp(
        jnp.arange(half_dim, dtype=jnp.float32) * (-2.0 * math.log(THETA) / vectors.shape[-1])
    )
    angles = offset.astype(jnp.float32)[:, None] * frequency[None, :]
    cosine = jnp.cos(angles)[:, None, :]
    sine_table = jnp.sin(angles)[:, None, :]
    first_half = vectors[..., :half_dim]
    second_half = vectors[..., half_dim:]
    return jnp.concatenate(
        [
            first_half * cosine - second_half * sine_table,
            second_half * cosine + first_half * sine_table,
        ],
        axis=-1,
    )


def adapter_terms(row_block, code_rows, a_in, pieces):
    table_count, rank_cols, in_width = a_in.shape
    projected = lax.dot_general(
        row_block,
        a_in.reshape(table_count * rank_cols, in_width),
        (((1,), (1,)), ((), ())),
        preferred_element_type=jnp.float32,
    )
    chosen = (jnp.arange(table_count, dtype=jnp.int32)[None, :] == code_rows[:, None]).astype(
        jnp.float32
    )
    low_rank = (projected.reshape(-1, table_count, rank_cols) * chosen[:, :, None]).astype(
        jnp.bfloat16
    )
    results = []
    for col_start, b_table in pieces:
        width_rank = b_table.shape[1]
        section = low_rank[:, :, col_start : col_start + width_rank].reshape(
            -1, table_count * width_rank
        )
        results.append(
            jnp.dot(
                section,
                b_table.reshape(table_count * width_rank, b_table.shape[2]),
                preferred_element_type=jnp.float32,
            ).astype(jnp.bfloat16)
        )
    return tuple(results)


def attention_kernel(block_count, query_ref, *refs):
    value_refs = refs[:block_count]
    query_segment_ref, key_segment_ref, out_ref = refs[block_count:]
    rows = query_ref.shape[0]
    keys = block_count * rows
    groups = HEADS // KV_HEADS
    query_segment = query_segment_ref[...]
    row_index = lax.broadcasted_iota(jnp.int32, (rows, keys), 0)
    col_index = lax.broadcasted_iota(jnp.int32, (rows, keys), 1)
    allowed = (query_segment == key_segment_ref[...]) & (col_index <= row_index + (keys - rows))
    allowed = jnp.concatenate([allowed] * groups, axis=0)
    for kv_head in range(KV_HEADS):
        key_cols = slice(kv_head * HEAD_WIDTH, (kv_head + 1) * HEAD_WIDTH)
        value_cols = slice(KVW + kv_head * HEAD_WIDTH, KVW + (kv_head + 1) * HEAD_WIDTH)
        key_head = jnp.concatenate([ref[:, key_cols] for ref in value_refs], axis=0)
        value_head = jnp.concatenate([ref[:, value_cols] for ref in value_refs], axis=0)
        query_group = jnp.concatenate(
            [
                query_ref[:, (kv_head * groups + group) * HEAD_WIDTH : (kv_head * groups + group + 1) * HEAD_WIDTH]
                for group in range(groups)
            ],
            axis=0,
        )
        scores = lax.dot_general(
            query_group, key_head, (((1,), (1,)), ((), ())), preferred_element_type=jnp.float32
        ) * HEAD_WIDTH ** (-0.5)
        scores = jnp.where(allowed, scores, -1e30)
        top_score = jnp.max(scores, axis=1, keepdims=True)
        exp_scores = jnp.exp(scores - top_score)
        row_total = jnp.sum(exp_scores, axis=1, keepdims=True)
        summed = jnp.dot(
            exp_scores.astype(jnp.bfloat16), value_head, preferred_element_type=jnp.float32
        )
        attended = (summed / row_total).astype(out_ref.dtype)
        for group in range(groups):
            head = kv_head * groups + group
            out_ref[:, head * HEAD_WIDTH : (head + 1) * HEAD_WIDTH] = attended[
                group * rows : (group + 1) * rows
            ]


def attend_blocks(queries, blocks, query_segment, key_segment):
    rows = queries.shape[0]
    block_count = len(blocks)
    keys = block_count * rows
    vmem = pl.BlockSpec(memory_space=pltpu.VMEM)
    return pl.pallas_call(
        functools.partial(attention_kernel, block_count),
        out_shape=jax.ShapeDtypeStruct(queries.shape, jnp.bfloat16),
        in_specs=[vmem] * (block_count + 3),
        out_specs=vmem,
        cost_estimate=pl.CostEstimate(
            flops=4 * HEADS * rows * keys * HEAD_WIDTH,
            transcendentals=HEADS * rows * keys,
            bytes_accessed=2 * (2 * queries.size + block_count * blocks[0].size),
        ),
    )(queries, *blocks, query_segment.reshape(rows, 1), key_segment.reshape(1, keys))


def on_device(
    tokens,
    norm_gain,
    w_query,
    w_key,
    w_value,
    w_output,
    qkv_in,
    q_out,
    kv_out,
    o_in,
    o_out,
    lengths,
    prompt_adapter,
    adapter_slot,
):
    tok_rows = tokens.shape[0]
    tok_count = lax.axis_size("tok")
    own_count = lax.axis_size("own")
    per_owner = qkv_in.shape[0]
    device_here = lax.axis_index(("tok", "own"))
    positions = device_here * tok_rows + jnp.arange(tok_rows, dtype=jnp.int32)
    segment, offset, members = prompt_index(positions, lengths)
    prompt_count = lengths.shape[0]
    first_segment = segment[0]
    code_rows = segment - first_segment
    normed = rms_norm(tokens, norm_gain)
    tables = (qkv_in, q_out, kv_out, o_in, o_out)
    table_shapes = tuple((table.shape[1:] for table in tables))
    packed = jnp.concatenate([table.reshape(per_owner, -1) for table in tables], axis=1)
    all_slots = lax.all_gather(packed, "own", axis=0, tiled=True)
    own_here = lax.axis_index("own")
    group_blocks = jnp.arange(tok_count, dtype=jnp.int32) * own_count + own_here
    prompt_starts = jnp.cumsum(lengths) - lengths
    group_first = (
        jnp.sum(
            (group_blocks[:, None] * tok_rows >= prompt_starts[None, :]).astype(jnp.int32), axis=1
        )
        - 1
    )
    group_segments = jnp.minimum(
        group_first[:, None] + jnp.arange(SEG_DEV, dtype=jnp.int32)[None, :], prompt_count - 1
    )
    group_adapter = jnp.sum(
        jnp.where(
            group_segments[:, :, None] == jnp.arange(prompt_count, dtype=jnp.int32)[None, None, :],
            prompt_adapter[None, None, :],
            0,
        ),
        axis=2,
    )
    group_slots = jnp.sum(
        jnp.where(
            group_adapter[:, :, None]
            == jnp.arange(adapter_slot.shape[0], dtype=jnp.int32)[None, None, :],
            adapter_slot[None, None, :],
            0,
        ),
        axis=2,
    )
    pick = (
        group_slots.reshape(-1)[:, None]
        == jnp.arange(all_slots.shape[0], dtype=jnp.int32)[None, :]
    ).astype(all_slots.dtype)
    outgoing = (
        jnp.dot(pick, all_slots, preferred_element_type=jnp.float32)
        .astype(all_slots.dtype)
        .reshape(tok_count, SEG_DEV, packed.shape[1])
    )
    split_col = sum(shape[0] * shape[1] for shape in table_shapes[:3])
    incoming = jnp.concatenate(
        [
            lax.all_to_all(outgoing[:, :, :split_col], "tok", 0, 0, tiled=True),
            lax.all_to_all(outgoing[:, :, split_col:], "tok", 0, 0, tiled=True),
        ],
        axis=2,
    )
    selected = []
    col = 0
    for table_shape in table_shapes:
        width = table_shape[0] * table_shape[1]
        piece = incoming[:, :, col : col + width].reshape(
            tok_count, SEG_DEV, table_shape[0], table_shape[1]
        )
        col += width
        selected.append(
            jnp.transpose(piece, (1, 2, 0, 3)).reshape(
                SEG_DEV, table_shape[0], tok_count * table_shape[1]
            )
        )
    input_maps, query_maps, keyvalue_maps, output_in_maps, output_out_maps = selected
    delta_q, delta_k, delta_v = adapter_terms(
        normed,
        code_rows,
        input_maps,
        ((0, query_maps), (RANK, keyvalue_maps[:, :RANK]), (2 * RANK, keyvalue_maps[:, RANK:])),
    )
    base_q = jnp.dot(normed, w_query, preferred_element_type=jnp.float32)
    base_k = jnp.dot(normed, w_key, preferred_element_type=jnp.float32)
    base_v = jnp.dot(normed, w_value, preferred_element_type=jnp.float32)
    query_lin = (base_q + delta_q.astype(jnp.float32)).reshape(tok_rows, HEADS, HEAD_WIDTH)
    queries = rotate(query_lin, offset).reshape(tok_rows, D).astype(jnp.bfloat16)
    key_lin = (base_k + delta_k.astype(jnp.float32)).reshape(tok_rows, KV_HEADS, HEAD_WIDTH)
    key_rows = rotate(key_lin, offset).reshape(tok_rows, KVW).astype(jnp.bfloat16)
    value_rows = (base_v + delta_v.astype(jnp.float32)).astype(jnp.bfloat16)
    key_value = jnp.concatenate([key_rows, value_rows], axis=1)

    earlier = [from_behind(key_value, ("tok", "own"), distance) for distance in range(REACH, 0, -1)]
    key_positions = (
        device_here * tok_rows
        - REACH * tok_rows
        + jnp.arange((REACH + 1) * tok_rows, dtype=jnp.int32)
    )
    key_segment = prompt_index(key_positions, lengths)[0]
    attn_rows = attend_blocks(queries, earlier + [key_value], segment, key_segment)
    delta_o = adapter_terms(attn_rows, code_rows, output_in_maps, ((0, output_out_maps),))[0]
    projected_out = jnp.dot(
        attn_rows, w_output, preferred_element_type=jnp.float32
    ) + delta_o.astype(jnp.float32)
    mixed_rows = (tokens.astype(jnp.float32) + projected_out).astype(jnp.bfloat16)
    return (mixed_rows, key_value)


def solution(mesh):
    return jax.shard_map(
        on_device,
        mesh=mesh,
        in_specs=(
            P(("tok", "own"), None),
            P(),
            P(),
            P(),
            P(),
            P(),
            P("own", None, "tok"),
            P("own", None, "tok"),
            P("own", None, "tok"),
            P("own", None, "tok"),
            P("own", None, "tok"),
            P(),
            P(),
            P(),
        ),
        out_specs=(P(("tok", "own"), None), P(("tok", "own"), None)),
        check_vma=False,
    )
```

```python
import math

import functools

import jax
import jax.numpy as jnp
from jax import lax
from jax.experimental import pallas as pl
from jax.experimental.pallas import tpu as pltpu
from jax.sharding import PartitionSpec as P

D = 1152
HEADS = 18
KV_HEADS = 6
HEAD_WIDTH = 64
RANK = 16
REACH = 12
KVW = 384
SEG_DEV = 5


EPS = 1e-05
THETA = 10000.0


def from_behind(block, axis, distance):
    devices = range(lax.axis_size(axis))
    route = [(i - distance, i) for i in devices if i - distance in devices]
    return lax.ppermute(block, axis, route)


def rms_norm(row_block, gain_vec):
    widened = row_block.astype(jnp.float32)
    inverse_rms = lax.rsqrt(jnp.mean(widened * widened, axis=-1, keepdims=True) + EPS)
    return (widened * inverse_rms * gain_vec.astype(jnp.float32)).astype(jnp.bfloat16)


def prompt_index(positions, lengths):
    prompt_ends = jnp.cumsum(lengths)
    prompt_starts = prompt_ends - lengths
    inside = (positions[:, None] >= prompt_starts[None, :]).astype(jnp.int32)
    segment = jnp.sum(inside, axis=1) - 1
    members = jnp.arange(lengths.shape[0], dtype=jnp.int32)[None, :] == segment[:, None]
    offset = positions - jnp.sum(jnp.where(members, prompt_starts[None, :], 0), axis=1)
    return (segment, offset, members)


def slot_lookup(adapter, adapter_slot):
    matches = jnp.arange(adapter_slot.shape[0], dtype=jnp.int32)[None, :] == adapter[:, None]
    return jnp.sum(jnp.where(matches, adapter_slot[None, :], 0), axis=1)


def rotate(vectors, offset):
    half_dim = vectors.shape[-1] // 2
    frequency = jnp.exp(
        jnp.arange(half_dim, dtype=jnp.float32) * (-2.0 * math.log(THETA) / vectors.shape[-1])
    )
    angles = offset.astype(jnp.float32)[:, None] * frequency[None, :]
    cosine = jnp.cos(angles)[:, None, :]
    sine_table = jnp.sin(angles)[:, None, :]
    first_half = vectors[..., :half_dim]
    second_half = vectors[..., half_dim:]
    return jnp.concatenate(
        [
            first_half * cosine - second_half * sine_table,
            second_half * cosine + first_half * sine_table,
        ],
        axis=-1,
    )


def adapter_terms(row_block, code_rows, a_in, pieces):
    table_count, rank_cols, in_width = a_in.shape
    projected = lax.dot_general(
        row_block,
        a_in.reshape(table_count * rank_cols, in_width),
        (((1,), (1,)), ((), ())),
        preferred_element_type=jnp.float32,
    )
    chosen = (jnp.arange(table_count, dtype=jnp.int32)[None, :] == code_rows[:, None]).astype(
        jnp.float32
    )
    low_rank = (projected.reshape(-1, table_count, rank_cols) * chosen[:, :, None]).astype(
        jnp.bfloat16
    )
    results = []
    for col_start, b_table in pieces:
        width_rank = b_table.shape[1]
        section = low_rank[:, :, col_start : col_start + width_rank].reshape(
            -1, table_count * width_rank
        )
        results.append(
            jnp.dot(
                section,
                b_table.reshape(table_count * width_rank, b_table.shape[2]),
                preferred_element_type=jnp.float32,
            ).astype(jnp.bfloat16)
        )
    return tuple(results)


def attention_kernel(block_count, query_ref, *refs):
    value_refs = refs[:block_count]
    query_segment_ref, key_segment_ref, out_ref = refs[block_count:]
    rows = query_ref.shape[0]
    keys = block_count * rows
    groups = HEADS // KV_HEADS
    query_segment = query_segment_ref[...]
    row_index = lax.broadcasted_iota(jnp.int32, (rows, keys), 0)
    col_index = lax.broadcasted_iota(jnp.int32, (rows, keys), 1)
    allowed = (query_segment == key_segment_ref[...]) & (col_index <= row_index + (keys - rows))
    allowed = jnp.concatenate([allowed] * groups, axis=0)
    for kv_head in range(KV_HEADS):
        key_cols = slice(kv_head * HEAD_WIDTH, (kv_head + 1) * HEAD_WIDTH)
        value_cols = slice(KVW + kv_head * HEAD_WIDTH, KVW + (kv_head + 1) * HEAD_WIDTH)
        key_head = jnp.concatenate([ref[:, key_cols] for ref in value_refs], axis=0)
        value_head = jnp.concatenate([ref[:, value_cols] for ref in value_refs], axis=0)
        query_group = jnp.concatenate(
            [
                query_ref[:, (kv_head * groups + group) * HEAD_WIDTH : (kv_head * groups + group + 1) * HEAD_WIDTH]
                for group in range(groups)
            ],
            axis=0,
        )
        scores = lax.dot_general(
            query_group, key_head, (((1,), (1,)), ((), ())), preferred_element_type=jnp.float32
        ) * HEAD_WIDTH ** (-0.5)
        scores = jnp.where(allowed, scores, -1e30)
        top_score = jnp.max(scores, axis=1, keepdims=True)
        exp_scores = jnp.exp(scores - top_score)
        row_total = jnp.sum(exp_scores, axis=1, keepdims=True)
        summed = jnp.dot(
            exp_scores.astype(jnp.bfloat16), value_head, preferred_element_type=jnp.float32
        )
        attended = (summed / row_total).astype(out_ref.dtype)
        for group in range(groups):
            head = kv_head * groups + group
            out_ref[:, head * HEAD_WIDTH : (head + 1) * HEAD_WIDTH] = attended[
                group * rows : (group + 1) * rows
            ]


def attend_blocks(queries, blocks, query_segment, key_segment):
    rows = queries.shape[0]
    block_count = len(blocks)
    keys = block_count * rows
    vmem = pl.BlockSpec(memory_space=pltpu.VMEM)
    return pl.pallas_call(
        functools.partial(attention_kernel, block_count),
        out_shape=jax.ShapeDtypeStruct(queries.shape, jnp.bfloat16),
        in_specs=[vmem] * (block_count + 3),
        out_specs=vmem,
        cost_estimate=pl.CostEstimate(
            flops=4 * HEADS * rows * keys * HEAD_WIDTH,
            transcendentals=HEADS * rows * keys,
            bytes_accessed=2 * (2 * queries.size + block_count * blocks[0].size),
        ),
    )(queries, *blocks, query_segment.reshape(rows, 1), key_segment.reshape(1, keys))


def on_device(
    tokens,
    norm_gain,
    w_query,
    w_key,
    w_value,
    w_output,
    qkv_in,
    q_out,
    kv_out,
    o_in,
    o_out,
    lengths,
    prompt_adapter,
    adapter_slot,
):
    tok_rows = tokens.shape[0]
    tok_count = lax.axis_size("tok")
    own_count = lax.axis_size("own")
    per_owner = qkv_in.shape[0]
    device_here = lax.axis_index(("tok", "own"))
    positions = device_here * tok_rows + jnp.arange(tok_rows, dtype=jnp.int32)
    segment, offset, members = prompt_index(positions, lengths)
    prompt_count = lengths.shape[0]
    first_segment = segment[0]
    code_rows = segment - first_segment
    normed = rms_norm(tokens, norm_gain)
    tables = (qkv_in, q_out, kv_out, o_in, o_out)
    table_shapes = tuple((table.shape[1:] for table in tables))
    packed = jnp.concatenate([table.reshape(per_owner, -1) for table in tables], axis=1)
    all_slots = lax.all_gather(packed, "own", axis=0, tiled=True)
    own_here = lax.axis_index("own")
    group_blocks = jnp.arange(tok_count, dtype=jnp.int32) * own_count + own_here
    prompt_starts = jnp.cumsum(lengths) - lengths
    group_first = (
        jnp.sum(
            (group_blocks[:, None] * tok_rows >= prompt_starts[None, :]).astype(jnp.int32), axis=1
        )
        - 1
    )
    group_segments = jnp.minimum(
        group_first[:, None] + jnp.arange(SEG_DEV, dtype=jnp.int32)[None, :], prompt_count - 1
    )
    group_adapter = jnp.sum(
        jnp.where(
            group_segments[:, :, None] == jnp.arange(prompt_count, dtype=jnp.int32)[None, None, :],
            prompt_adapter[None, None, :],
            0,
        ),
        axis=2,
    )
    group_slots = jnp.sum(
        jnp.where(
            group_adapter[:, :, None]
            == jnp.arange(adapter_slot.shape[0], dtype=jnp.int32)[None, None, :],
            adapter_slot[None, None, :],
            0,
        ),
        axis=2,
    )
    pick = (
        group_slots.T.reshape(-1)[:, None]
        == jnp.arange(all_slots.shape[0], dtype=jnp.int32)[None, :]
    ).astype(all_slots.dtype)
    split_col = sum(shape[0] * shape[1] for shape in table_shapes[:3])
    parts = (
        (slice(0, split_col), table_shapes[:3]),
        (slice(split_col, packed.shape[1]), table_shapes[3:]),
    )
    selected = []
    for cols, shapes in parts:
        outgoing = (
            jnp.dot(pick, all_slots[:, cols], preferred_element_type=jnp.float32)
            .astype(all_slots.dtype)
            .reshape(SEG_DEV, tok_count, cols.stop - cols.start)
        )
        incoming = lax.all_to_all(outgoing, "tok", 1, 1, tiled=True)
        col = 0
        for table_shape in shapes:
            width = table_shape[0] * table_shape[1]
            piece = incoming[:, :, col : col + width].reshape(
                SEG_DEV, tok_count, table_shape[0], table_shape[1]
            )
            col += width
            selected.append(
                jnp.transpose(piece, (0, 2, 1, 3)).reshape(
                    SEG_DEV, table_shape[0], tok_count * table_shape[1]
                )
            )
    input_maps, query_maps, keyvalue_maps, output_in_maps, output_out_maps = selected
    delta_q, delta_k, delta_v = adapter_terms(
        normed,
        code_rows,
        input_maps,
        ((0, query_maps), (RANK, keyvalue_maps[:, :RANK]), (2 * RANK, keyvalue_maps[:, RANK:])),
    )
    base_q = jnp.dot(normed, w_query, preferred_element_type=jnp.float32)
    base_k = jnp.dot(normed, w_key, preferred_element_type=jnp.float32)
    base_v = jnp.dot(normed, w_value, preferred_element_type=jnp.float32)
    query_lin = (base_q + delta_q.astype(jnp.float32)).reshape(tok_rows, HEADS, HEAD_WIDTH)
    queries = rotate(query_lin, offset).reshape(tok_rows, D).astype(jnp.bfloat16)
    key_lin = (base_k + delta_k.astype(jnp.float32)).reshape(tok_rows, KV_HEADS, HEAD_WIDTH)
    key_rows = rotate(key_lin, offset).reshape(tok_rows, KVW).astype(jnp.bfloat16)
    value_rows = (base_v + delta_v.astype(jnp.float32)).astype(jnp.bfloat16)
    key_value = jnp.concatenate([key_rows, value_rows], axis=1)

    earlier = [from_behind(key_value, ("tok", "own"), distance) for distance in range(REACH, 0, -1)]
    key_positions = (
        device_here * tok_rows
        - REACH * tok_rows
        + jnp.arange((REACH + 1) * tok_rows, dtype=jnp.int32)
    )
    key_segment = prompt_index(key_positions, lengths)[0]
    attn_rows = attend_blocks(queries, earlier + [key_value], segment, key_segment)
    delta_o = adapter_terms(attn_rows, code_rows, output_in_maps, ((0, output_out_maps),))[0]
    projected_out = jnp.dot(
        attn_rows, w_output, preferred_element_type=jnp.float32
    ) + delta_o.astype(jnp.float32)
    mixed_rows = (tokens.astype(jnp.float32) + projected_out).astype(jnp.bfloat16)
    return (mixed_rows, key_value)


def solution(mesh):
    return jax.shard_map(
        on_device,
        mesh=mesh,
        in_specs=(
            P(("tok", "own"), None),
            P(),
            P(),
            P(),
            P(),
            P(),
            P("own", None, "tok"),
            P("own", None, "tok"),
            P("own", None, "tok"),
            P("own", None, "tok"),
            P("own", None, "tok"),
            P(),
            P(),
            P(),
        ),
        out_specs=(P(("tok", "own"), None), P(("tok", "own"), None)),
        check_vma=False,
    )
```

```python
import math

import functools

import jax
import jax.numpy as jnp
from jax import lax
from jax.experimental import pallas as pl
from jax.experimental.pallas import tpu as pltpu
from jax.sharding import PartitionSpec as P

D = 1152
HEADS = 18
KV_HEADS = 6
HEAD_WIDTH = 64
RANK = 16
REACH = 12
KVW = 384
SEG_DEV = 5


EPS = 1e-05
THETA = 10000.0


def from_behind(block, axis, distance):
    devices = range(lax.axis_size(axis))
    route = [(i - distance, i) for i in devices if i - distance in devices]
    return lax.ppermute(block, axis, route)


def rms_norm(row_block, gain_vec):
    widened = row_block.astype(jnp.float32)
    inverse_rms = lax.rsqrt(jnp.mean(widened * widened, axis=-1, keepdims=True) + EPS)
    return (widened * inverse_rms * gain_vec.astype(jnp.float32)).astype(jnp.bfloat16)


def prompt_index(positions, lengths):
    prompt_ends = jnp.cumsum(lengths)
    prompt_starts = prompt_ends - lengths
    inside = (positions[:, None] >= prompt_starts[None, :]).astype(jnp.int32)
    segment = jnp.sum(inside, axis=1) - 1
    members = jnp.arange(lengths.shape[0], dtype=jnp.int32)[None, :] == segment[:, None]
    offset = positions - jnp.sum(jnp.where(members, prompt_starts[None, :], 0), axis=1)
    return (segment, offset, members)


def slot_lookup(adapter, adapter_slot):
    matches = jnp.arange(adapter_slot.shape[0], dtype=jnp.int32)[None, :] == adapter[:, None]
    return jnp.sum(jnp.where(matches, adapter_slot[None, :], 0), axis=1)


def rotate(vectors, offset):
    half_dim = vectors.shape[-1] // 2
    frequency = jnp.exp(
        jnp.arange(half_dim, dtype=jnp.float32) * (-2.0 * math.log(THETA) / vectors.shape[-1])
    )
    angles = offset.astype(jnp.float32)[:, None] * frequency[None, :]
    cosine = jnp.cos(angles)[:, None, :]
    sine_table = jnp.sin(angles)[:, None, :]
    first_half = vectors[..., :half_dim]
    second_half = vectors[..., half_dim:]
    return jnp.concatenate(
        [
            first_half * cosine - second_half * sine_table,
            second_half * cosine + first_half * sine_table,
        ],
        axis=-1,
    )


def adapter_terms(row_block, code_rows, a_in, pieces):
    table_count, rank_cols, in_width = a_in.shape
    projected = lax.dot_general(
        row_block,
        a_in.reshape(table_count * rank_cols, in_width),
        (((1,), (1,)), ((), ())),
        preferred_element_type=jnp.float32,
    )
    chosen = (jnp.arange(table_count, dtype=jnp.int32)[None, :] == code_rows[:, None]).astype(
        jnp.float32
    )
    low_rank = (projected.reshape(-1, table_count, rank_cols) * chosen[:, :, None]).astype(
        jnp.bfloat16
    )
    results = []
    for col_start, b_table in pieces:
        width_rank = b_table.shape[1]
        section = low_rank[:, :, col_start : col_start + width_rank].reshape(
            -1, table_count * width_rank
        )
        results.append(
            jnp.dot(
                section,
                b_table.reshape(table_count * width_rank, b_table.shape[2]),
                preferred_element_type=jnp.float32,
            ).astype(jnp.bfloat16)
        )
    return tuple(results)


def attention_kernel(block_count, query_ref, *refs):
    value_refs = refs[:block_count]
    query_segment_ref, key_segment_ref, out_ref = refs[block_count:]
    rows = query_ref.shape[0]
    keys = block_count * rows
    groups = HEADS // KV_HEADS
    query_segment = query_segment_ref[...]
    row_index = lax.broadcasted_iota(jnp.int32, (rows, keys), 0)
    col_index = lax.broadcasted_iota(jnp.int32, (rows, keys), 1)
    allowed = (query_segment == key_segment_ref[...]) & (col_index <= row_index + (keys - rows))
    allowed = jnp.concatenate([allowed] * groups, axis=0)
    for kv_head in range(KV_HEADS):
        key_cols = slice(kv_head * HEAD_WIDTH, (kv_head + 1) * HEAD_WIDTH)
        value_cols = slice(KVW + kv_head * HEAD_WIDTH, KVW + (kv_head + 1) * HEAD_WIDTH)
        key_head = jnp.concatenate([ref[:, key_cols] for ref in value_refs], axis=0)
        value_head = jnp.concatenate([ref[:, value_cols] for ref in value_refs], axis=0)
        query_group = jnp.concatenate(
            [
                query_ref[:, (kv_head * groups + group) * HEAD_WIDTH : (kv_head * groups + group + 1) * HEAD_WIDTH]
                for group in range(groups)
            ],
            axis=0,
        )
        scores = lax.dot_general(
            query_group, key_head, (((1,), (1,)), ((), ())), preferred_element_type=jnp.float32
        ) * HEAD_WIDTH ** (-0.5)
        scores = jnp.where(allowed, scores, -1e30)
        top_score = jnp.max(scores, axis=1, keepdims=True)
        exp_scores = jnp.exp(scores - top_score)
        row_total = jnp.sum(exp_scores, axis=1, keepdims=True)
        summed = jnp.dot(
            exp_scores.astype(jnp.bfloat16), value_head, preferred_element_type=jnp.float32
        )
        attended = (summed / row_total).astype(out_ref.dtype)
        for group in range(groups):
            head = kv_head * groups + group
            out_ref[:, head * HEAD_WIDTH : (head + 1) * HEAD_WIDTH] = attended[
                group * rows : (group + 1) * rows
            ]


def attend_blocks(queries, blocks, query_segment, key_segment):
    rows = queries.shape[0]
    block_count = len(blocks)
    keys = block_count * rows
    vmem = pl.BlockSpec(memory_space=pltpu.VMEM)
    return pl.pallas_call(
        functools.partial(attention_kernel, block_count),
        out_shape=jax.ShapeDtypeStruct(queries.shape, jnp.bfloat16),
        in_specs=[vmem] * (block_count + 3),
        out_specs=vmem,
        cost_estimate=pl.CostEstimate(
            flops=4 * HEADS * rows * keys * HEAD_WIDTH,
            transcendentals=HEADS * rows * keys,
            bytes_accessed=2 * (2 * queries.size + block_count * blocks[0].size),
        ),
    )(queries, *blocks, query_segment.reshape(rows, 1), key_segment.reshape(1, keys))


def on_device(
    tokens,
    norm_gain,
    w_query,
    w_key,
    w_value,
    w_output,
    qkv_in,
    q_out,
    kv_out,
    o_in,
    o_out,
    lengths,
    prompt_adapter,
    adapter_slot,
):
    tok_rows = tokens.shape[0]
    tok_count = lax.axis_size("tok")
    own_count = lax.axis_size("own")
    per_owner = qkv_in.shape[0]
    device_here = lax.axis_index(("tok", "own"))
    positions = device_here * tok_rows + jnp.arange(tok_rows, dtype=jnp.int32)
    segment, offset, members = prompt_index(positions, lengths)
    prompt_count = lengths.shape[0]
    first_segment = segment[0]
    code_rows = segment - first_segment
    normed = rms_norm(tokens, norm_gain)
    tables = (qkv_in, q_out, kv_out, o_in, o_out)
    table_shapes = tuple((table.shape[1:] for table in tables))
    packed = jnp.concatenate([table.reshape(per_owner, -1) for table in tables], axis=1)
    all_slots = lax.all_gather(packed, "own", axis=0, tiled=True)
    own_here = lax.axis_index("own")
    group_blocks = jnp.arange(tok_count, dtype=jnp.int32) * own_count + own_here
    prompt_starts = jnp.cumsum(lengths) - lengths
    group_first = (
        jnp.sum(
            (group_blocks[:, None] * tok_rows >= prompt_starts[None, :]).astype(jnp.int32), axis=1
        )
        - 1
    )
    group_segments = jnp.minimum(
        group_first[:, None] + jnp.arange(SEG_DEV, dtype=jnp.int32)[None, :], prompt_count - 1
    )
    group_adapter = jnp.sum(
        jnp.where(
            group_segments[:, :, None] == jnp.arange(prompt_count, dtype=jnp.int32)[None, None, :],
            prompt_adapter[None, None, :],
            0,
        ),
        axis=2,
    )
    group_slots = jnp.sum(
        jnp.where(
            group_adapter[:, :, None]
            == jnp.arange(adapter_slot.shape[0], dtype=jnp.int32)[None, None, :],
            adapter_slot[None, None, :],
            0,
        ),
        axis=2,
    )
    pick = (
        group_slots.T.reshape(-1)[:, None]
        == jnp.arange(all_slots.shape[0], dtype=jnp.int32)[None, :]
    ).astype(all_slots.dtype)
    split_col = sum(shape[0] * shape[1] for shape in table_shapes[:3])
    parts = (
        (slice(0, split_col), table_shapes[:3]),
        (slice(split_col, packed.shape[1]), table_shapes[3:]),
    )
    selected = []
    for cols, shapes in parts:
        outgoing = (
            jnp.dot(pick, all_slots[:, cols], preferred_element_type=jnp.float32)
            .astype(all_slots.dtype)
            .reshape(SEG_DEV, tok_count, cols.stop - cols.start)
        )
        incoming = lax.all_to_all(outgoing, "tok", 1, 1, tiled=True)
        runs = []
        for table_shape in shapes:
            if runs and runs[-1][0][1] == table_shape[1]:
                runs[-1].append(table_shape)
            else:
                runs.append([table_shape])
        col = 0
        for run in runs:
            run_rows = sum(shape[0] for shape in run)
            run_width = run[0][1]
            piece = incoming[:, :, col : col + run_rows * run_width].reshape(
                SEG_DEV, tok_count, run_rows, run_width
            )
            col += run_rows * run_width
            full = jnp.transpose(piece, (0, 2, 1, 3)).reshape(
                SEG_DEV, run_rows, tok_count * run_width
            )
            row = 0
            for shape in run:
                selected.append(full[:, row : row + shape[0]])
                row += shape[0]
    input_maps, query_maps, keyvalue_maps, output_in_maps, output_out_maps = selected
    delta_q, delta_k, delta_v = adapter_terms(
        normed,
        code_rows,
        input_maps,
        ((0, query_maps), (RANK, keyvalue_maps[:, :RANK]), (2 * RANK, keyvalue_maps[:, RANK:])),
    )
    base_q = jnp.dot(normed, w_query, preferred_element_type=jnp.float32)
    base_k = jnp.dot(normed, w_key, preferred_element_type=jnp.float32)
    base_v = jnp.dot(normed, w_value, preferred_element_type=jnp.float32)
    query_lin = (base_q + delta_q.astype(jnp.float32)).reshape(tok_rows, HEADS, HEAD_WIDTH)
    queries = rotate(query_lin, offset).reshape(tok_rows, D).astype(jnp.bfloat16)
    key_lin = (base_k + delta_k.astype(jnp.float32)).reshape(tok_rows, KV_HEADS, HEAD_WIDTH)
    key_rows = rotate(key_lin, offset).reshape(tok_rows, KVW).astype(jnp.bfloat16)
    value_rows = (base_v + delta_v.astype(jnp.float32)).astype(jnp.bfloat16)
    key_value = jnp.concatenate([key_rows, value_rows], axis=1)

    earlier = [from_behind(key_value, ("tok", "own"), distance) for distance in range(REACH, 0, -1)]
    key_positions = (
        device_here * tok_rows
        - REACH * tok_rows
        + jnp.arange((REACH + 1) * tok_rows, dtype=jnp.int32)
    )
    key_segment = prompt_index(key_positions, lengths)[0]
    attn_rows = attend_blocks(queries, earlier + [key_value], segment, key_segment)
    delta_o = adapter_terms(attn_rows, code_rows, output_in_maps, ((0, output_out_maps),))[0]
    projected_out = jnp.dot(
        attn_rows, w_output, preferred_element_type=jnp.float32
    ) + delta_o.astype(jnp.float32)
    mixed_rows = (tokens.astype(jnp.float32) + projected_out).astype(jnp.bfloat16)
    return (mixed_rows, key_value)


def solution(mesh):
    return jax.shard_map(
        on_device,
        mesh=mesh,
        in_specs=(
            P(("tok", "own"), None),
            P(),
            P(),
            P(),
            P(),
            P(),
            P("own", None, "tok"),
            P("own", None, "tok"),
            P("own", None, "tok"),
            P("own", None, "tok"),
            P("own", None, "tok"),
            P(),
            P(),
            P(),
        ),
        out_specs=(P(("tok", "own"), None), P(("tok", "own"), None)),
        check_vma=False,
    )
```

```python
import math

import functools

import jax
import jax.numpy as jnp
from jax import lax
from jax.experimental import pallas as pl
from jax.experimental.pallas import tpu as pltpu
from jax.sharding import PartitionSpec as P

D = 1152
HEADS = 18
KV_HEADS = 6
HEAD_WIDTH = 64
RANK = 16
REACH = 12
KVW = 384
SEG_DEV = 5


EPS = 1e-05
THETA = 10000.0


def from_behind(block, axis, distance):
    devices = range(lax.axis_size(axis))
    route = [(i - distance, i) for i in devices if i - distance in devices]
    return lax.ppermute(block, axis, route)


def rms_norm(row_block, gain_vec):
    widened = row_block.astype(jnp.float32)
    inverse_rms = lax.rsqrt(jnp.mean(widened * widened, axis=-1, keepdims=True) + EPS)
    return (widened * inverse_rms * gain_vec.astype(jnp.float32)).astype(jnp.bfloat16)


def prompt_index(positions, lengths):
    prompt_ends = jnp.cumsum(lengths)
    prompt_starts = prompt_ends - lengths
    inside = (positions[:, None] >= prompt_starts[None, :]).astype(jnp.int32)
    segment = jnp.sum(inside, axis=1) - 1
    members = jnp.arange(lengths.shape[0], dtype=jnp.int32)[None, :] == segment[:, None]
    offset = positions - jnp.sum(jnp.where(members, prompt_starts[None, :], 0), axis=1)
    return (segment, offset, members)


def slot_lookup(adapter, adapter_slot):
    matches = jnp.arange(adapter_slot.shape[0], dtype=jnp.int32)[None, :] == adapter[:, None]
    return jnp.sum(jnp.where(matches, adapter_slot[None, :], 0), axis=1)


def rotate(vectors, offset):
    half_dim = vectors.shape[-1] // 2
    frequency = jnp.exp(
        jnp.arange(half_dim, dtype=jnp.float32) * (-2.0 * math.log(THETA) / vectors.shape[-1])
    )
    angles = offset.astype(jnp.float32)[:, None] * frequency[None, :]
    cosine = jnp.cos(angles)[:, None, :]
    sine_table = jnp.sin(angles)[:, None, :]
    first_half = vectors[..., :half_dim]
    second_half = vectors[..., half_dim:]
    return jnp.concatenate(
        [
            first_half * cosine - second_half * sine_table,
            second_half * cosine + first_half * sine_table,
        ],
        axis=-1,
    )


def adapter_terms(row_block, code_rows, a_in, pieces):
    table_count, rank_cols, in_width = a_in.shape
    projected = lax.dot_general(
        row_block,
        a_in.reshape(table_count * rank_cols, in_width),
        (((1,), (1,)), ((), ())),
        preferred_element_type=jnp.float32,
    )
    chosen = (jnp.arange(table_count, dtype=jnp.int32)[None, :] == code_rows[:, None]).astype(
        jnp.float32
    )
    low_rank = (projected.reshape(-1, table_count, rank_cols) * chosen[:, :, None]).astype(
        jnp.bfloat16
    )
    results = []
    for col_start, b_table in pieces:
        width_rank = b_table.shape[1]
        section = low_rank[:, :, col_start : col_start + width_rank].reshape(
            -1, table_count * width_rank
        )
        results.append(
            jnp.dot(
                section,
                b_table.reshape(table_count * width_rank, b_table.shape[2]),
                preferred_element_type=jnp.float32,
            ).astype(jnp.bfloat16)
        )
    return tuple(results)


def attention_kernel(block_count, query_ref, *refs):
    value_refs = refs[:block_count]
    (
        query_segment_ref,
        key_segment_ref,
        tokens_ref,
        w_output_ref,
        o_in_ref,
        o_out_ref,
        chosen_ref,
        mixed_ref,
        out_ref,
    ) = refs[block_count:]
    rows = query_ref.shape[0]
    keys = block_count * rows
    groups = HEADS // KV_HEADS
    query_segment = query_segment_ref[...]
    row_index = lax.broadcasted_iota(jnp.int32, (rows, keys), 0)
    col_index = lax.broadcasted_iota(jnp.int32, (rows, keys), 1)
    allowed = (query_segment == key_segment_ref[...]) & (col_index <= row_index + (keys - rows))
    allowed = jnp.concatenate([allowed] * groups, axis=0)
    for kv_head in range(KV_HEADS):
        key_cols = slice(kv_head * HEAD_WIDTH, (kv_head + 1) * HEAD_WIDTH)
        value_cols = slice(KVW + kv_head * HEAD_WIDTH, KVW + (kv_head + 1) * HEAD_WIDTH)
        key_head = jnp.concatenate([ref[:, key_cols] for ref in value_refs], axis=0)
        value_head = jnp.concatenate([ref[:, value_cols] for ref in value_refs], axis=0)
        query_group = jnp.concatenate(
            [
                query_ref[:, (kv_head * groups + group) * HEAD_WIDTH : (kv_head * groups + group + 1) * HEAD_WIDTH]
                for group in range(groups)
            ],
            axis=0,
        )
        scores = lax.dot_general(
            query_group, key_head, (((1,), (1,)), ((), ())), preferred_element_type=jnp.float32
        ) * HEAD_WIDTH ** (-0.5)
        scores = jnp.where(allowed, scores, -1e30)
        top_score = jnp.max(scores, axis=1, keepdims=True)
        exp_scores = jnp.exp(scores - top_score)
        row_total = jnp.sum(exp_scores, axis=1, keepdims=True)
        summed = jnp.dot(
            exp_scores.astype(jnp.bfloat16), value_head, preferred_element_type=jnp.float32
        )
        attended = (summed / row_total).astype(out_ref.dtype)
        for group in range(groups):
            head = kv_head * groups + group
            out_ref[:, head * HEAD_WIDTH : (head + 1) * HEAD_WIDTH] = attended[
                group * rows : (group + 1) * rows
            ]
    attended_rows = out_ref[...]
    low_o = lax.dot_general(
        attended_rows, o_in_ref[...], (((1,), (1,)), ((), ())), preferred_element_type=jnp.float32
    )
    low_o = (low_o * chosen_ref[...]).astype(jnp.bfloat16)
    delta_o = jnp.dot(low_o, o_out_ref[...], preferred_element_type=jnp.float32).astype(
        jnp.bfloat16
    )
    projected_out = jnp.dot(
        attended_rows, w_output_ref[...], preferred_element_type=jnp.float32
    ) + delta_o.astype(jnp.float32)
    mixed_ref[...] = (tokens_ref[...].astype(jnp.float32) + projected_out).astype(mixed_ref.dtype)


def attend_blocks(queries, blocks, query_segment, key_segment, tokens, w_output, o_in, o_out, chosen):
    rows = queries.shape[0]
    block_count = len(blocks)
    keys = sum(block.shape[0] for block in blocks)
    vmem = pl.BlockSpec(memory_space=pltpu.VMEM)
    return pl.pallas_call(
        functools.partial(attention_kernel, block_count),
        out_shape=jax.ShapeDtypeStruct(tokens.shape, tokens.dtype),
        in_specs=[vmem] * (block_count + 8),
        out_specs=vmem,
        scratch_shapes=[pltpu.VMEM(queries.shape, jnp.bfloat16)],
        cost_estimate=pl.CostEstimate(
            flops=4 * HEADS * rows * keys * HEAD_WIDTH + 2 * rows * D * (D + 4 * o_in.shape[0]),
            transcendentals=HEADS * rows * keys,
            bytes_accessed=2 * (3 * queries.size + keys * blocks[0].shape[1] + w_output.size),
        ),
        compiler_params=pltpu.CompilerParams(vmem_limit_bytes=48 * 1024 * 1024),
    )(
        queries,
        *blocks,
        query_segment.reshape(rows, 1),
        key_segment.reshape(1, keys),
        tokens,
        w_output,
        o_in,
        o_out,
        chosen,
    )


def on_device(
    tokens,
    norm_gain,
    w_query,
    w_key,
    w_value,
    w_output,
    qkv_in,
    q_out,
    kv_out,
    o_in,
    o_out,
    lengths,
    prompt_adapter,
    adapter_slot,
):
    tok_rows = tokens.shape[0]
    tok_count = lax.axis_size("tok")
    own_count = lax.axis_size("own")
    per_owner = qkv_in.shape[0]
    device_here = lax.axis_index(("tok", "own"))
    positions = device_here * tok_rows + jnp.arange(tok_rows, dtype=jnp.int32)
    segment, offset, members = prompt_index(positions, lengths)
    prompt_count = lengths.shape[0]
    first_segment = segment[0]
    code_rows = segment - first_segment
    normed = rms_norm(tokens, norm_gain)
    tables = (qkv_in, q_out, kv_out, o_in, o_out)
    table_shapes = tuple((table.shape[1:] for table in tables))
    packed = jnp.concatenate([table.reshape(per_owner, -1) for table in tables], axis=1)
    all_slots = lax.all_gather(packed, "own", axis=0, tiled=True)
    own_here = lax.axis_index("own")
    group_blocks = jnp.arange(tok_count, dtype=jnp.int32) * own_count + own_here
    prompt_starts = jnp.cumsum(lengths) - lengths
    group_first = (
        jnp.sum(
            (group_blocks[:, None] * tok_rows >= prompt_starts[None, :]).astype(jnp.int32), axis=1
        )
        - 1
    )
    group_segments = jnp.minimum(
        group_first[:, None] + jnp.arange(SEG_DEV, dtype=jnp.int32)[None, :], prompt_count - 1
    )
    group_adapter = jnp.sum(
        jnp.where(
            group_segments[:, :, None] == jnp.arange(prompt_count, dtype=jnp.int32)[None, None, :],
            prompt_adapter[None, None, :],
            0,
        ),
        axis=2,
    )
    group_slots = jnp.sum(
        jnp.where(
            group_adapter[:, :, None]
            == jnp.arange(adapter_slot.shape[0], dtype=jnp.int32)[None, None, :],
            adapter_slot[None, None, :],
            0,
        ),
        axis=2,
    )
    pick = (
        group_slots.T.reshape(-1)[:, None]
        == jnp.arange(all_slots.shape[0], dtype=jnp.int32)[None, :]
    ).astype(all_slots.dtype)
    split_col = sum(shape[0] * shape[1] for shape in table_shapes[:3])
    parts = (
        (slice(0, split_col), table_shapes[:3]),
        (slice(split_col, packed.shape[1]), table_shapes[3:]),
    )
    selected = []
    for cols, shapes in parts:
        outgoing = (
            jnp.dot(pick, all_slots[:, cols], preferred_element_type=jnp.float32)
            .astype(all_slots.dtype)
            .reshape(SEG_DEV, tok_count, cols.stop - cols.start)
        )
        incoming = lax.all_to_all(outgoing, "tok", 1, 1, tiled=True)
        col = 0
        for table_shape in shapes:
            width = table_shape[0] * table_shape[1]
            piece = incoming[:, :, col : col + width].reshape(
                SEG_DEV, tok_count, table_shape[0], table_shape[1]
            )
            col += width
            selected.append(
                jnp.transpose(piece, (0, 2, 1, 3)).reshape(
                    SEG_DEV, table_shape[0], tok_count * table_shape[1]
                )
            )
    input_maps, query_maps, keyvalue_maps, output_in_maps, output_out_maps = selected
    delta_q, delta_k, delta_v = adapter_terms(
        normed,
        code_rows,
        input_maps,
        ((0, query_maps), (RANK, keyvalue_maps[:, :RANK]), (2 * RANK, keyvalue_maps[:, RANK:])),
    )
    base_q = jnp.dot(normed, w_query, preferred_element_type=jnp.float32)
    base_k = jnp.dot(normed, w_key, preferred_element_type=jnp.float32)
    base_v = jnp.dot(normed, w_value, preferred_element_type=jnp.float32)
    query_lin = (base_q + delta_q.astype(jnp.float32)).reshape(tok_rows, HEADS, HEAD_WIDTH)
    queries = rotate(query_lin, offset).reshape(tok_rows, D).astype(jnp.bfloat16)
    key_lin = (base_k + delta_k.astype(jnp.float32)).reshape(tok_rows, KV_HEADS, HEAD_WIDTH)
    key_rows = rotate(key_lin, offset).reshape(tok_rows, KVW).astype(jnp.bfloat16)
    value_rows = (base_v + delta_v.astype(jnp.float32)).astype(jnp.bfloat16)
    key_value = jnp.concatenate([key_rows, value_rows], axis=1)

    earlier = [from_behind(key_value, ("tok", "own"), distance) for distance in range(REACH, 0, -1)]
    key_positions = (
        device_here * tok_rows
        - REACH * tok_rows
        + jnp.arange((REACH + 1) * tok_rows, dtype=jnp.int32)
    )
    key_segment = prompt_index(key_positions, lengths)[0]
    rank_rows = output_in_maps.shape[1]
    chosen = jnp.repeat(
        (jnp.arange(SEG_DEV, dtype=jnp.int32)[None, :] == code_rows[:, None]).astype(jnp.float32),
        rank_rows,
        axis=1,
    )
    mixed_rows = attend_blocks(
        queries,
        earlier + [key_value],
        segment,
        key_segment,
        tokens,
        w_output,
        output_in_maps.reshape(SEG_DEV * rank_rows, -1),
        output_out_maps.reshape(SEG_DEV * rank_rows, -1),
        chosen,
    )
    return (mixed_rows, key_value)


def solution(mesh):
    return jax.shard_map(
        on_device,
        mesh=mesh,
        in_specs=(
            P(("tok", "own"), None),
            P(),
            P(),
            P(),
            P(),
            P(),
            P("own", None, "tok"),
            P("own", None, "tok"),
            P("own", None, "tok"),
            P("own", None, "tok"),
            P("own", None, "tok"),
            P(),
            P(),
            P(),
        ),
        out_specs=(P(("tok", "own"), None), P(("tok", "own"), None)),
        check_vma=False,
    )
```

```python
import math

import functools

import jax
import jax.numpy as jnp
from jax import lax
from jax.experimental import pallas as pl
from jax.experimental.pallas import tpu as pltpu
from jax.sharding import PartitionSpec as P

D = 1152
HEADS = 18
KV_HEADS = 6
HEAD_WIDTH = 64
RANK = 16
REACH = 12
KVW = 384
SEG_DEV = 5


EPS = 1e-05
THETA = 10000.0


def from_behind(block, axis, distance):
    devices = range(lax.axis_size(axis))
    route = [(i - distance, i) for i in devices if i - distance in devices]
    return lax.ppermute(block, axis, route)


def rms_norm(row_block, gain_vec):
    widened = row_block.astype(jnp.float32)
    inverse_rms = lax.rsqrt(jnp.mean(widened * widened, axis=-1, keepdims=True) + EPS)
    return (widened * inverse_rms * gain_vec.astype(jnp.float32)).astype(jnp.bfloat16)


def prompt_index(positions, lengths):
    prompt_ends = jnp.cumsum(lengths)
    prompt_starts = prompt_ends - lengths
    inside = (positions[:, None] >= prompt_starts[None, :]).astype(jnp.int32)
    segment = jnp.sum(inside, axis=1) - 1
    members = jnp.arange(lengths.shape[0], dtype=jnp.int32)[None, :] == segment[:, None]
    offset = positions - jnp.sum(jnp.where(members, prompt_starts[None, :], 0), axis=1)
    return (segment, offset, members)


def slot_lookup(adapter, adapter_slot):
    matches = jnp.arange(adapter_slot.shape[0], dtype=jnp.int32)[None, :] == adapter[:, None]
    return jnp.sum(jnp.where(matches, adapter_slot[None, :], 0), axis=1)


def rotate(vectors, offset):
    half_dim = vectors.shape[-1] // 2
    frequency = jnp.exp(
        jnp.arange(half_dim, dtype=jnp.float32) * (-2.0 * math.log(THETA) / vectors.shape[-1])
    )
    angles = offset.astype(jnp.float32)[:, None] * frequency[None, :]
    cosine = jnp.cos(angles)[:, None, :]
    sine_table = jnp.sin(angles)[:, None, :]
    first_half = vectors[..., :half_dim]
    second_half = vectors[..., half_dim:]
    return jnp.concatenate(
        [
            first_half * cosine - second_half * sine_table,
            second_half * cosine + first_half * sine_table,
        ],
        axis=-1,
    )


def adapter_terms(row_block, code_rows, a_in, pieces):
    table_count, rank_cols, in_width = a_in.shape
    projected = lax.dot_general(
        row_block,
        a_in.reshape(table_count * rank_cols, in_width),
        (((1,), (1,)), ((), ())),
        preferred_element_type=jnp.float32,
    )
    chosen = (jnp.arange(table_count, dtype=jnp.int32)[None, :] == code_rows[:, None]).astype(
        jnp.float32
    )
    low_rank = (projected.reshape(-1, table_count, rank_cols) * chosen[:, :, None]).astype(
        jnp.bfloat16
    )
    results = []
    for col_start, b_table in pieces:
        width_rank = b_table.shape[1]
        section = low_rank[:, :, col_start : col_start + width_rank].reshape(
            -1, table_count * width_rank
        )
        results.append(
            jnp.dot(
                section,
                b_table.reshape(table_count * width_rank, b_table.shape[2]),
                preferred_element_type=jnp.float32,
            ).astype(jnp.bfloat16)
        )
    return tuple(results)


def attention_kernel(block_count, query_ref, *refs):
    value_refs = refs[:block_count]
    (
        query_segment_ref,
        key_segment_ref,
        tokens_ref,
        w_output_ref,
        o_in_ref,
        o_out_ref,
        chosen_ref,
        mixed_ref,
        out_ref,
        w_output_vmem,
        copy_sem,
    ) = refs[block_count:]
    w_output_copy = pltpu.make_async_copy(w_output_ref, w_output_vmem, copy_sem)
    w_output_copy.start()
    rows = query_ref.shape[0]
    keys = block_count * rows
    groups = HEADS // KV_HEADS
    query_segment = query_segment_ref[...]
    row_index = lax.broadcasted_iota(jnp.int32, (rows, keys), 0)
    col_index = lax.broadcasted_iota(jnp.int32, (rows, keys), 1)
    allowed = (query_segment == key_segment_ref[...]) & (col_index <= row_index + (keys - rows))
    allowed = jnp.concatenate([allowed] * groups, axis=0)
    for kv_head in range(KV_HEADS):
        key_cols = slice(kv_head * HEAD_WIDTH, (kv_head + 1) * HEAD_WIDTH)
        value_cols = slice(KVW + kv_head * HEAD_WIDTH, KVW + (kv_head + 1) * HEAD_WIDTH)
        key_head = jnp.concatenate([ref[:, key_cols] for ref in value_refs], axis=0)
        value_head = jnp.concatenate([ref[:, value_cols] for ref in value_refs], axis=0)
        query_group = jnp.concatenate(
            [
                query_ref[:, (kv_head * groups + group) * HEAD_WIDTH : (kv_head * groups + group + 1) * HEAD_WIDTH]
                for group in range(groups)
            ],
            axis=0,
        )
        scores = lax.dot_general(
            query_group, key_head, (((1,), (1,)), ((), ())), preferred_element_type=jnp.float32
        ) * HEAD_WIDTH ** (-0.5)
        scores = jnp.where(allowed, scores, -1e30)
        top_score = jnp.max(scores, axis=1, keepdims=True)
        exp_scores = jnp.exp(scores - top_score)
        row_total = jnp.sum(exp_scores, axis=1, keepdims=True)
        summed = jnp.dot(
            exp_scores.astype(jnp.bfloat16), value_head, preferred_element_type=jnp.float32
        )
        attended = (summed / row_total).astype(out_ref.dtype)
        for group in range(groups):
            head = kv_head * groups + group
            out_ref[:, head * HEAD_WIDTH : (head + 1) * HEAD_WIDTH] = attended[
                group * rows : (group + 1) * rows
            ]
    attended_rows = out_ref[...]
    low_o = lax.dot_general(
        attended_rows, o_in_ref[...], (((1,), (1,)), ((), ())), preferred_element_type=jnp.float32
    )
    low_o = (low_o * chosen_ref[...]).astype(jnp.bfloat16)
    delta_o = jnp.dot(low_o, o_out_ref[...], preferred_element_type=jnp.float32).astype(
        jnp.bfloat16
    )
    w_output_copy.wait()
    projected_out = jnp.dot(
        attended_rows, w_output_vmem[...], preferred_element_type=jnp.float32
    ) + delta_o.astype(jnp.float32)
    mixed_ref[...] = (tokens_ref[...].astype(jnp.float32) + projected_out).astype(mixed_ref.dtype)


def attend_blocks(queries, blocks, query_segment, key_segment, tokens, w_output, o_in, o_out, chosen):
    rows = queries.shape[0]
    block_count = len(blocks)
    keys = sum(block.shape[0] for block in blocks)
    vmem = pl.BlockSpec(memory_space=pltpu.VMEM)
    return pl.pallas_call(
        functools.partial(attention_kernel, block_count),
        out_shape=jax.ShapeDtypeStruct(tokens.shape, tokens.dtype),
        in_specs=[vmem] * (block_count + 4) + [pl.BlockSpec(memory_space=pl.ANY)] + [vmem] * 3,
        out_specs=vmem,
        scratch_shapes=[
            pltpu.VMEM(queries.shape, jnp.bfloat16),
            pltpu.VMEM(w_output.shape, w_output.dtype),
            pltpu.SemaphoreType.DMA(()),
        ],
        cost_estimate=pl.CostEstimate(
            flops=4 * HEADS * rows * keys * HEAD_WIDTH + 2 * rows * D * (D + 4 * o_in.shape[0]),
            transcendentals=HEADS * rows * keys,
            bytes_accessed=2 * (3 * queries.size + keys * blocks[0].shape[1] + w_output.size),
        ),
        compiler_params=pltpu.CompilerParams(vmem_limit_bytes=48 * 1024 * 1024),
    )(
        queries,
        *blocks,
        query_segment.reshape(rows, 1),
        key_segment.reshape(1, keys),
        tokens,
        w_output,
        o_in,
        o_out,
        chosen,
    )


def on_device(
    tokens,
    norm_gain,
    w_query,
    w_key,
    w_value,
    w_output,
    qkv_in,
    q_out,
    kv_out,
    o_in,
    o_out,
    lengths,
    prompt_adapter,
    adapter_slot,
):
    tok_rows = tokens.shape[0]
    tok_count = lax.axis_size("tok")
    own_count = lax.axis_size("own")
    per_owner = qkv_in.shape[0]
    device_here = lax.axis_index(("tok", "own"))
    positions = device_here * tok_rows + jnp.arange(tok_rows, dtype=jnp.int32)
    segment, offset, members = prompt_index(positions, lengths)
    prompt_count = lengths.shape[0]
    first_segment = segment[0]
    code_rows = segment - first_segment
    normed = rms_norm(tokens, norm_gain)
    tables = (qkv_in, q_out, kv_out, o_in, o_out)
    table_shapes = tuple((table.shape[1:] for table in tables))
    packed = jnp.concatenate([table.reshape(per_owner, -1) for table in tables], axis=1)
    all_slots = lax.all_gather(packed, "own", axis=0, tiled=True)
    own_here = lax.axis_index("own")
    group_blocks = jnp.arange(tok_count, dtype=jnp.int32) * own_count + own_here
    prompt_starts = jnp.cumsum(lengths) - lengths
    group_first = (
        jnp.sum(
            (group_blocks[:, None] * tok_rows >= prompt_starts[None, :]).astype(jnp.int32), axis=1
        )
        - 1
    )
    group_segments = jnp.minimum(
        group_first[:, None] + jnp.arange(SEG_DEV, dtype=jnp.int32)[None, :], prompt_count - 1
    )
    group_adapter = jnp.sum(
        jnp.where(
            group_segments[:, :, None] == jnp.arange(prompt_count, dtype=jnp.int32)[None, None, :],
            prompt_adapter[None, None, :],
            0,
        ),
        axis=2,
    )
    group_slots = jnp.sum(
        jnp.where(
            group_adapter[:, :, None]
            == jnp.arange(adapter_slot.shape[0], dtype=jnp.int32)[None, None, :],
            adapter_slot[None, None, :],
            0,
        ),
        axis=2,
    )
    pick = (
        group_slots.T.reshape(-1)[:, None]
        == jnp.arange(all_slots.shape[0], dtype=jnp.int32)[None, :]
    ).astype(all_slots.dtype)
    split_col = sum(shape[0] * shape[1] for shape in table_shapes[:3])
    parts = (
        (slice(0, split_col), table_shapes[:3]),
        (slice(split_col, packed.shape[1]), table_shapes[3:]),
    )
    selected = []
    for cols, shapes in parts:
        outgoing = (
            jnp.dot(pick, all_slots[:, cols], preferred_element_type=jnp.float32)
            .astype(all_slots.dtype)
            .reshape(SEG_DEV, tok_count, cols.stop - cols.start)
        )
        incoming = lax.all_to_all(outgoing, "tok", 1, 1, tiled=True)
        col = 0
        for table_shape in shapes:
            width = table_shape[0] * table_shape[1]
            piece = incoming[:, :, col : col + width].reshape(
                SEG_DEV, tok_count, table_shape[0], table_shape[1]
            )
            col += width
            selected.append(
                jnp.transpose(piece, (0, 2, 1, 3)).reshape(
                    SEG_DEV, table_shape[0], tok_count * table_shape[1]
                )
            )
    input_maps, query_maps, keyvalue_maps, output_in_maps, output_out_maps = selected
    delta_q, delta_k, delta_v = adapter_terms(
        normed,
        code_rows,
        input_maps,
        ((0, query_maps), (RANK, keyvalue_maps[:, :RANK]), (2 * RANK, keyvalue_maps[:, RANK:])),
    )
    base_q = jnp.dot(normed, w_query, preferred_element_type=jnp.float32)
    base_k = jnp.dot(normed, w_key, preferred_element_type=jnp.float32)
    base_v = jnp.dot(normed, w_value, preferred_element_type=jnp.float32)
    query_lin = (base_q + delta_q.astype(jnp.float32)).reshape(tok_rows, HEADS, HEAD_WIDTH)
    queries = rotate(query_lin, offset).reshape(tok_rows, D).astype(jnp.bfloat16)
    key_lin = (base_k + delta_k.astype(jnp.float32)).reshape(tok_rows, KV_HEADS, HEAD_WIDTH)
    key_rows = rotate(key_lin, offset).reshape(tok_rows, KVW).astype(jnp.bfloat16)
    value_rows = (base_v + delta_v.astype(jnp.float32)).astype(jnp.bfloat16)
    key_value = jnp.concatenate([key_rows, value_rows], axis=1)

    earlier = [from_behind(key_value, ("tok", "own"), distance) for distance in range(REACH, 0, -1)]
    key_positions = (
        device_here * tok_rows
        - REACH * tok_rows
        + jnp.arange((REACH + 1) * tok_rows, dtype=jnp.int32)
    )
    key_segment = prompt_index(key_positions, lengths)[0]
    rank_rows = output_in_maps.shape[1]
    chosen = jnp.repeat(
        (jnp.arange(SEG_DEV, dtype=jnp.int32)[None, :] == code_rows[:, None]).astype(jnp.float32),
        rank_rows,
        axis=1,
    )
    mixed_rows = attend_blocks(
        queries,
        earlier + [key_value],
        segment,
        key_segment,
        tokens,
        w_output,
        output_in_maps.reshape(SEG_DEV * rank_rows, -1),
        output_out_maps.reshape(SEG_DEV * rank_rows, -1),
        chosen,
    )
    return (mixed_rows, key_value)


def solution(mesh):
    return jax.shard_map(
        on_device,
        mesh=mesh,
        in_specs=(
            P(("tok", "own"), None),
            P(),
            P(),
            P(),
            P(),
            P(),
            P("own", None, "tok"),
            P("own", None, "tok"),
            P("own", None, "tok"),
            P("own", None, "tok"),
            P("own", None, "tok"),
            P(),
            P(),
            P(),
        ),
        out_specs=(P(("tok", "own"), None), P(("tok", "own"), None)),
        check_vma=False,
    )
```
